512 devices in a mesh: cluster: 128 (over z, y, x_lo), feat: 4 (over x_hi, core).
Axes of the slice: x: 4 (x_hi: 2, x_lo: 2; x = x_hi * 2 + x_lo), y: 4, z: 16, core: 2. Of those that a mesh axis runs over, the one named last changes fastest.
Arguments:
- queries: bfloat16 [32768, 1024], P('cluster', 'feat'), may hold values from -6 to 6
- assign: int32 [32768, 1], P('cluster'), may hold values from 0 to 127, as said below
- band_mask: int32 [128, 7], replicated, may hold values from 0 to 1, as said below
- keys: bfloat16 [65536, 1024], P(('cluster', 'feat')), may hold values from -6 to 6
- labels: bfloat16 [65536, 1000], P(('cluster', 'feat')), may hold values from -24 to 24
- prior: bfloat16 [65536], P(('cluster', 'feat')), may hold values from -2 to 506
Outputs:
- propagated: bfloat16 [32768, 1000], P('cluster', 'feat')
The draws below stay inside these ranges and needn't reach their ends.
Inputs may be any that keep to these rules, and one draw needn't show every extreme that they name: `assign`: in each aligned block of 256 rows at most 4 rows name one cluster. `band_mask`: entry 3 of every row is 1.
All inputs are finite; a program needn't handle non-finite values.
Results may differ from the reference program's by a relative error of at most 0.014.
Values may be sent and summed in bfloat16 or wider, within the bound.
No kernel may reach another device: no remote copies, remote signals or barrier semaphores. Data moves between devices by JAX's collectives and lax.ppermute only.
A program may use at most 64 MiB of HBM per device.

```python
import math
import jax
import jax.numpy as jnp
from jax import lax

D = 1024
CLASSES = 1000
Q_DEV = 256
CB = 128
REACH = 3
BAND = 7
CLUSTERS = 128
CAP = 4
QUERIES = 32768
CORPUS = 65536


def key_table(key):
    return jnp.clip(jax.random.normal(jax.random.fold_in(key, 11), (CORPUS, D), jnp.float32), -6.0, 6.0)


def mask_table(key):
    coins = jax.random.randint(jax.random.fold_in(key, 13), (CLUSTERS, BAND), 0, 4)
    centre = jnp.arange(BAND)[None, :] == REACH
    return jnp.where(centre | (coins > 0), 1, 0).astype(jnp.int32)


def assign_block(block_key):
    hottest = jax.random.randint(jax.random.fold_in(block_key, 1), (), 0, CLUSTERS)
    order = jax.random.permutation(jax.random.fold_in(block_key, 2), CLUSTERS * CAP)
    owner = order // CAP
    ranked = jnp.where(owner == hottest, CLUSTERS * CAP, 0) + jnp.arange(CLUSTERS * CAP)
    others = owner[jnp.argsort(ranked)][:Q_DEV - CAP]
    rows_all = jnp.concatenate([jnp.full((CAP,), hottest, jnp.int32), others.astype(jnp.int32)])
    shuffle = jax.random.permutation(jax.random.fold_in(block_key, 3), Q_DEV)
    return rows_all[shuffle]


def assign_table(key):
    block_keys = jax.random.split(jax.random.fold_in(key, 31), CLUSTERS)
    return jax.vmap(assign_block)(block_keys).reshape(QUERIES).astype(jnp.int32)


def draw_band_mask(key, part):
    return mask_table(key)


def draw_assign(key, part):
    return assign_table(key).reshape(QUERIES, 1)


def draw_keys(key, part):
    return key_table(key).astype(jnp.bfloat16)


def draw_queries(key, part):
    base = jnp.clip(jax.random.normal(jax.random.fold_in(key, 41), (QUERIES, D), jnp.float32), -6.0, 6.0)
    home = assign_table(key)
    band_table = mask_table(key)
    picked = jax.random.randint(jax.random.fold_in(key, 43), (QUERIES,), 0, BAND)
    alive = band_table[home, picked] > 0
    offset = jnp.where(alive, picked, REACH) - REACH
    cluster = (home + offset) % CLUSTERS
    per_cluster = CORPUS // CLUSTERS
    device = jax.random.randint(jax.random.fold_in(key, 47), (QUERIES,), 0, per_cluster // CB)
    row_index = (cluster * per_cluster + device * CB).astype(jnp.int32)
    aligned = jnp.clip(3.0 * key_table(key)[row_index], -6.0, 6.0)
    chosen = jax.random.randint(jax.random.fold_in(key, 53), (QUERIES,), 0, 8) == 0
    return jnp.where(chosen[:, None], aligned, base).astype(jnp.bfloat16)


def draw_prior(key, part):
    base = jnp.clip(jax.random.normal(jax.random.fold_in(key, 51), (CORPUS,), jnp.float32) * 0.6, -2.0, 2.0)
    return base.astype(jnp.bfloat16)


def steps_of(rng, extent, cuts, least, top_value):
    gain, own = 1.0, jax.random.fold_in(rng, 6)
    for dim, parts in cuts:
        steps = jnp.exp(jax.random.uniform(jax.random.fold_in(own, dim), (parts,), jnp.float32, least / len(cuts), top_value / len(cuts)))
        gain = gain * jnp.repeat(steps, extent[dim] // parts).reshape([-1 if axis == dim else 1 for axis in range(len(extent))])
    return gain


def noise(own_key, dims, deviation, limit, shards=(), kind=jnp.bfloat16):
    result = jax.random.normal(own_key, dims, jnp.float32) * deviation
    if len(shards) > 0:
        result = steps_of(own_key, dims, shards, -0.22, 0.18) * result
    return jnp.clip(result, min=-limit, max=limit).astype(kind)


def setup_inputs(seed: int = 0) -> dict:
    arg_keys = jax.random.split(jax.random.key(seed), 7)
    queries = draw_queries(jax.random.fold_in(arg_keys[6], 71), 0)
    assign = draw_assign(jax.random.fold_in(arg_keys[6], 71), 0)
    band_mask = draw_band_mask(jax.random.fold_in(arg_keys[6], 71), 0)
    keys = draw_keys(jax.random.fold_in(arg_keys[6], 71), 0)
    labels = noise(arg_keys[4], (CORPUS, CLASSES), 4.0, 24.0, ((0, 512),))
    prior = draw_prior(jax.random.fold_in(arg_keys[6], 71), 0)
    return {"queries": queries, "assign": assign, "band_mask": band_mask, "keys": keys, "labels": labels, "prior": prior}


def reference(queries, assign, band_mask, keys, labels, prior):
    capacity = 2 * Q_DEV // CLUSTERS
    slots = CLUSTERS * capacity
    target = assign[:, 0].astype(jnp.int32)
    onehot = (target[:, None] == jnp.arange(CLUSTERS, dtype=jnp.int32)[None, :]).astype(jnp.int32)
    before = jnp.cumsum(onehot, axis=0) - onehot
    position = (target * slots + lax.optimization_barrier(jnp.sum(before * onehot, axis=1))).astype(jnp.int32)
    grouped = jnp.zeros((CLUSTERS * slots, D), queries.dtype).at[position].set(queries)
    grouped = grouped.reshape(CLUSTERS, slots, D)
    per_cluster = CORPUS // CLUSTERS
    key_blocks = keys.reshape(CLUSTERS, per_cluster, D)
    label_blocks = labels.reshape(CLUSTERS, per_cluster, CLASSES)
    prior_blocks = prior.reshape(CLUSTERS, per_cluster)
    offsets = jnp.arange(-REACH, REACH + 1, dtype=jnp.int32)
    scale = 2.0 / math.sqrt(D)

    def score_cluster(cluster):
        chosen = ((cluster + offsets) % CLUSTERS).astype(jnp.int32)
        band_keys = jnp.take(key_blocks, chosen, axis=0).reshape(BAND * per_cluster, D)
        band_labels = jnp.take(label_blocks, chosen, axis=0).reshape(BAND * per_cluster, CLASSES)
        band_prior = jnp.take(prior_blocks, chosen, axis=0).reshape(BAND * per_cluster)
        live = jnp.repeat(band_mask[cluster] > 0, per_cluster)
        scores = jnp.dot(grouped[cluster], band_keys.T, preferred_element_type=jnp.float32) * scale
        scores = scores + band_prior.astype(jnp.float32)[None, :]
        top = lax.optimization_barrier(jnp.max(jnp.where(live[None, :], scores, -jnp.inf), axis=1))
        weight = jnp.where(live[None, :], jnp.exp(scores - top[:, None]), jnp.float32(0.0))
        total = lax.optimization_barrier(jnp.sum(weight, axis=1))
        numer = jnp.dot(weight.astype(jnp.bfloat16), band_labels, preferred_element_type=jnp.float32)
        return (numer / total[:, None]).astype(jnp.bfloat16)
    results = lax.map(score_cluster, jnp.arange(CLUSTERS, dtype=jnp.int32))
    return results.reshape(CLUSTERS * slots, CLASSES)[position]
```

```python
import math

import jax
import jax.numpy as jnp
from jax import lax
from jax.sharding import PartitionSpec as P

REACH = 3


temper = 2.0


def shifted(array, axis, by):
    peers = lax.axis_size(axis)
    return lax.ppermute(array, axis, [(i, (i - by) % peers) for i in range(peers)])


def swapped(array, axis, bit):
    peers = lax.axis_size(axis)
    return lax.ppermute(array, axis, [(i, i ^ bit) for i in range(peers)])


def round_bf16(x):
    return lax.reduce_precision(x, exponent_bits=8, mantissa_bits=7)


def split3(x):
    hi = round_bf16(x)
    rest = x - hi
    mid = round_bf16(rest)
    lo = rest - mid
    return [part.astype(jnp.bfloat16) for part in (hi, mid, lo)]


def join3(parts):
    hi, mid, lo = [p.astype(jnp.float32) for p in parts]
    return (hi + mid) + lo


def pack(part, top, total, width):
    rows = part.shape[0]
    codes = split3(top) + split3(total)
    columns = [part.astype(jnp.bfloat16)] + [c[:, None] for c in codes]
    pad = width - part.shape[1] - len(codes)
    columns.append(jnp.zeros((rows, pad), jnp.bfloat16))
    return jnp.concatenate(columns, axis=1)


def merge(kept, top, total, message, width):
    other = message[:, :width].astype(jnp.float32)
    codes = [message[:, width + i] for i in range(6)]
    other_top = join3(codes[:3])
    other_total = join3(codes[3:])
    highest = jnp.maximum(top, other_top)
    mine = jnp.exp(top - highest)
    theirs = jnp.exp(other_top - highest)
    merged = kept * mine[:, None] + other * theirs[:, None]
    return merged, highest, total * mine + other_total * theirs


def body(queries, assign, band_mask, keys, labels, prior):
    clusters = lax.axis_size("cluster")
    cluster_index = lax.axis_index("cluster")
    feat_index = lax.axis_index("feat")
    local_rows = queries.shape[0]
    depth = keys.shape[1]
    classes = labels.shape[1]
    rows = keys.shape[0]
    capacity = 2 * local_rows // clusters
    slots = clusters * capacity

    width = depth + classes + 1
    padded = -(-width // 128) * 128
    block = jnp.concatenate(
        [keys, labels, prior[:, None], jnp.zeros((rows, padded - width), keys.dtype)], axis=1
    )
    offsets = [0]
    for reach in range(1, REACH + 1):
        offsets += [reach, -reach]
    blocks = [block] + [shifted(block, "cluster", o) for o in offsets[1:]]

    target = assign[:, 0]
    onehot = (target[:, None] == jnp.arange(clusters, dtype=jnp.int32)[None, :]).astype(jnp.int32)
    before = jnp.cumsum(onehot, axis=0) - onehot
    position = target * capacity + jnp.sum(before * onehot, axis=1)
    outgoing = jnp.zeros((slots, queries.shape[1]), queries.dtype).at[position].set(queries)
    arrived = lax.all_to_all(
        outgoing.reshape(clusters, capacity, queries.shape[1]),
        "cluster",
        split_axis=0,
        concat_axis=0,
        tiled=True,
    )
    query_full = lax.all_gather(
        arrived.reshape(slots, queries.shape[1]), "feat", axis=1, tiled=True
    )

    stacked = jnp.stack(blocks)
    band_keys = stacked[:, :, :depth].reshape(len(offsets) * rows, depth)
    band_labels = stacked[:, :, depth : depth + classes].reshape(len(offsets) * rows, classes)
    band_prior = stacked[:, :, depth + classes].reshape(len(offsets) * rows)
    mask_row = band_mask[cluster_index]
    live_blocks = jnp.stack([mask_row[REACH + o] > 0 for o in offsets])
    live = jnp.repeat(live_blocks, rows)
    scale = temper / math.sqrt(depth)
    scores = jnp.einsum("qd,kd->qk", query_full, band_keys, preferred_element_type=jnp.float32) * scale
    scores = scores + band_prior.astype(jnp.float32)[None, :]
    scores = jnp.where(live[None, :], scores, -jnp.inf)
    top = jnp.max(scores, axis=1)
    weight = jnp.exp(scores - top[:, None])
    total = jnp.sum(weight, axis=1)
    accum = jnp.dot(weight.astype(jnp.bfloat16), band_labels, preferred_element_type=jnp.float32)

    quarter = classes // 4
    core = feat_index % 2
    side = feat_index // 2
    grid = accum.reshape(slots, 2, 2, quarter)
    kept = lax.dynamic_index_in_dim(grid, core, axis=2, keepdims=False)
    sent = lax.dynamic_index_in_dim(grid, 1 - core, axis=2, keepdims=False)
    message = swapped(pack(sent.reshape(slots, 2 * quarter), top, total, 2 * quarter + 12), "feat", 1)
    kept, top, total = merge(kept.reshape(slots, 2 * quarter), top, total, message, 2 * quarter)
    grid = kept.reshape(slots, 2, quarter)
    kept = lax.dynamic_index_in_dim(grid, side, axis=1, keepdims=False)
    sent = lax.dynamic_index_in_dim(grid, 1 - side, axis=1, keepdims=False)
    message = swapped(pack(sent, top, total, quarter + 6), "feat", 2)
    kept, top, total = merge(kept, top, total, message, quarter)
    shares = (kept / total[:, None]).astype(jnp.bfloat16)

    returned = lax.all_to_all(
        shares.reshape(clusters, capacity, quarter),
        "cluster",
        split_axis=0,
        concat_axis=0,
        tiled=True,
    )
    return returned.reshape(slots, quarter)[position]


def solution(mesh):
    in_specs = (
        P("cluster", "feat"),
        P("cluster", None),
        P(),
        P(("cluster", "feat"), None),
        P(("cluster", "feat"), None),
        P(("cluster", "feat")),
    )
    out_specs = P("cluster", "feat")
    return jax.shard_map(body, mesh=mesh, in_specs=in_specs, out_specs=out_specs, check_vma=False)
```

```python
import math

import jax
import jax.numpy as jnp
from jax import lax
from jax.sharding import PartitionSpec as P

REACH = 3


temper = 2.0


def shifted(array, axis, by):
    peers = lax.axis_size(axis)
    return lax.ppermute(array, axis, [(i, (i - by) % peers) for i in range(peers)])


def swapped(array, axis, bit):
    peers = lax.axis_size(axis)
    return lax.ppermute(array, axis, [(i, i ^ bit) for i in range(peers)])


def round_bf16(x):
    return lax.reduce_precision(x, exponent_bits=8, mantissa_bits=7)


def split3(x):
    hi = round_bf16(x)
    rest = x - hi
    mid = round_bf16(rest)
    lo = rest - mid
    return [part.astype(jnp.bfloat16) for part in (hi, mid, lo)]


def join3(parts):
    hi, mid, lo = [p.astype(jnp.float32) for p in parts]
    return (hi + mid) + lo


def pack(part, top, total, width):
    rows = part.shape[0]
    codes = split3(top) + split3(total)
    columns = [part.astype(jnp.bfloat16)] + [c[:, None] for c in codes]
    pad = width - part.shape[1] - len(codes)
    columns.append(jnp.zeros((rows, pad), jnp.bfloat16))
    return jnp.concatenate(columns, axis=1)


def merge(kept, top, total, message, width):
    other = message[:, :width].astype(jnp.float32)
    codes = [message[:, width + i] for i in range(6)]
    other_top = join3(codes[:3])
    other_total = join3(codes[3:])
    highest = jnp.maximum(top, other_top)
    mine = jnp.exp(top - highest)
    theirs = jnp.exp(other_top - highest)
    merged = kept * mine[:, None] + other * theirs[:, None]
    return merged, highest, total * mine + other_total * theirs


def body(queries, assign, band_mask, keys, labels, prior):
    clusters = lax.axis_size("cluster")
    cluster_index = lax.axis_index("cluster")
    feat_index = lax.axis_index("feat")
    local_rows = queries.shape[0]
    depth = keys.shape[1]
    classes = labels.shape[1]
    rows = keys.shape[0]
    capacity = 2 * local_rows // clusters
    slots = clusters * capacity

    spare = depth - classes - 1
    block = jnp.stack(
        [keys, jnp.concatenate([labels, prior[:, None], jnp.zeros((rows, spare), keys.dtype)], axis=1)]
    )
    offsets = [0]
    for reach in range(1, REACH + 1):
        offsets += [reach, -reach]
    blocks = [block] + [shifted(block, "cluster", o) for o in offsets[1:]]

    target = assign[:, 0]
    onehot = (target[:, None] == jnp.arange(clusters, dtype=jnp.int32)[None, :]).astype(jnp.int32)
    before = jnp.cumsum(onehot, axis=0) - onehot
    position = target * capacity + jnp.sum(before * onehot, axis=1)
    outgoing = jnp.zeros((slots, queries.shape[1]), queries.dtype).at[position].set(queries)
    arrived = lax.all_to_all(
        outgoing.reshape(clusters, capacity, queries.shape[1]),
        "cluster",
        split_axis=0,
        concat_axis=0,
        tiled=True,
    )
    query_full = lax.all_gather(
        arrived.reshape(slots, queries.shape[1]), "feat", axis=1, tiled=True
    )

    mask_row = band_mask[cluster_index]
    live_blocks = jnp.stack([mask_row[REACH + o] > 0 for o in offsets])
    live = jnp.repeat(live_blocks, rows)
    scale = temper / math.sqrt(depth)
    scores = jnp.concatenate(
        [
            jnp.einsum("qd,kd->qk", query_full, b[0], preferred_element_type=jnp.float32) * scale
            + b[1][:, classes].astype(jnp.float32)[None, :]
            for b in blocks
        ],
        axis=1,
    )
    scores = jnp.where(live[None, :], scores, -jnp.inf)
    top = jnp.max(scores, axis=1)
    weight = jnp.exp(scores - top[:, None])
    total = jnp.sum(weight, axis=1)
    rounded = weight.astype(jnp.bfloat16)
    accum = sum(
        jnp.dot(rounded[:, i * rows : (i + 1) * rows], b[1], preferred_element_type=jnp.float32)
        for i, b in enumerate(blocks)
    )[:, :classes]

    quarter = classes // 4
    core = feat_index % 2
    side = feat_index // 2
    grid = accum.reshape(slots, 2, 2, quarter)
    kept = lax.dynamic_index_in_dim(grid, core, axis=2, keepdims=False)
    sent = lax.dynamic_index_in_dim(grid, 1 - core, axis=2, keepdims=False)
    message = swapped(pack(sent.reshape(slots, 2 * quarter), top, total, 2 * quarter + 12), "feat", 1)
    kept, top, total = merge(kept.reshape(slots, 2 * quarter), top, total, message, 2 * quarter)
    grid = kept.reshape(slots, 2, quarter)
    kept = lax.dynamic_index_in_dim(grid, side, axis=1, keepdims=False)
    sent = lax.dynamic_index_in_dim(grid, 1 - side, axis=1, keepdims=False)
    message = swapped(pack(sent, top, total, quarter + 6), "feat", 2)
    kept, top, total = merge(kept, top, total, message, quarter)
    shares = (kept / total[:, None]).astype(jnp.bfloat16)

    returned = lax.all_to_all(
        shares.reshape(clusters, capacity, quarter),
        "cluster",
        split_axis=0,
        concat_axis=0,
        tiled=True,
    )
    return returned.reshape(slots, quarter)[position]


def solution(mesh):
    in_specs = (
        P("cluster", "feat"),
        P("cluster", None),
        P(),
        P(("cluster", "feat"), None),
        P(("cluster", "feat"), None),
        P(("cluster", "feat")),
    )
    out_specs = P("cluster", "feat")
    return jax.shard_map(body, mesh=mesh, in_specs=in_specs, out_specs=out_specs, check_vma=False)
```

```python
import math

import jax
import jax.numpy as jnp
from jax import lax
from jax.sharding import Mesh
from jax.sharding import PartitionSpec as P

REACH = 3


temper = 2.0
CLUSTER = ("outer", "inner")


def routed(array, forward):
    outer = lax.axis_size("outer")
    inner = lax.axis_size("inner")
    tail = array.shape[1:]
    grid = array.reshape((outer, inner) + tail)
    stages = ("inner", "outer") if forward else ("outer", "inner")
    for axis in stages:
        if axis == "inner":
            grid = jnp.swapaxes(grid, 0, 1)
        grid = lax.all_to_all(grid, axis, split_axis=0, concat_axis=0, tiled=True)
        if axis == "inner":
            grid = jnp.swapaxes(grid, 0, 1)
    return grid.reshape(array.shape)


def shifted(array, axis, by):
    peers = lax.axis_size(axis)
    return lax.ppermute(array, axis, [(i, (i - by) % peers) for i in range(peers)])


def swapped(array, axis, bit):
    peers = lax.axis_size(axis)
    return lax.ppermute(array, axis, [(i, i ^ bit) for i in range(peers)])


def round_bf16(x):
    return lax.reduce_precision(x, exponent_bits=8, mantissa_bits=7)


def split3(x):
    hi = round_bf16(x)
    rest = x - hi
    mid = round_bf16(rest)
    lo = rest - mid
    return [part.astype(jnp.bfloat16) for part in (hi, mid, lo)]


def join3(parts):
    hi, mid, lo = [p.astype(jnp.float32) for p in parts]
    return (hi + mid) + lo


def pack(part, top, total, width):
    rows = part.shape[0]
    codes = split3(top) + split3(total)
    columns = [part.astype(jnp.bfloat16)] + [c[:, None] for c in codes]
    pad = width - part.shape[1] - len(codes)
    columns.append(jnp.zeros((rows, pad), jnp.bfloat16))
    return jnp.concatenate(columns, axis=1)


def merge(kept, top, total, message, width):
    other = message[:, :width].astype(jnp.float32)
    codes = [message[:, width + i] for i in range(6)]
    other_top = join3(codes[:3])
    other_total = join3(codes[3:])
    highest = jnp.maximum(top, other_top)
    mine = jnp.exp(top - highest)
    theirs = jnp.exp(other_top - highest)
    merged = kept * mine[:, None] + other * theirs[:, None]
    return merged, highest, total * mine + other_total * theirs


def body(queries, assign, band_mask, keys, labels, prior):
    clusters = lax.axis_size(CLUSTER)
    cluster_index = lax.axis_index(CLUSTER)
    feat_index = lax.axis_index("feat")
    local_rows = queries.shape[0]
    depth = keys.shape[1]
    classes = labels.shape[1]
    rows = keys.shape[0]
    capacity = 2 * local_rows // clusters
    slots = clusters * capacity

    width = depth + classes + 1
    padded = -(-width // 128) * 128
    block = jnp.concatenate(
        [keys, labels, prior[:, None], jnp.zeros((rows, padded - width), keys.dtype)], axis=1
    )
    offsets = [0]
    for reach in range(1, REACH + 1):
        offsets += [reach, -reach]
    blocks = [block] + [shifted(block, CLUSTER, o) for o in offsets[1:]]

    target = assign[:, 0]
    onehot = (target[:, None] == jnp.arange(clusters, dtype=jnp.int32)[None, :]).astype(jnp.int32)
    before = jnp.cumsum(onehot, axis=0) - onehot
    position = target * capacity + jnp.sum(before * onehot, axis=1)
    outgoing = jnp.zeros((slots, queries.shape[1]), queries.dtype).at[position].set(queries)
    arrived = routed(outgoing.reshape(clusters, capacity, queries.shape[1]), True)
    query_full = lax.all_gather(
        arrived.reshape(slots, queries.shape[1]), "feat", axis=1, tiled=True
    )

    stacked = jnp.stack(blocks)
    band_keys = stacked[:, :, :depth].reshape(len(offsets) * rows, depth)
    band_labels = stacked[:, :, depth : depth + classes].reshape(len(offsets) * rows, classes)
    band_prior = stacked[:, :, depth + classes].reshape(len(offsets) * rows)
    mask_row = band_mask[cluster_index]
    live_blocks = jnp.stack([mask_row[REACH + o] > 0 for o in offsets])
    live = jnp.repeat(live_blocks, rows)
    scale = temper / math.sqrt(depth)
    scores = jnp.einsum("qd,kd->qk", query_full, band_keys, preferred_element_type=jnp.float32) * scale
    scores = scores + band_prior.astype(jnp.float32)[None, :]
    scores = jnp.where(live[None, :], scores, -jnp.inf)
    top = jnp.max(scores, axis=1)
    weight = jnp.exp(scores - top[:, None])
    total = jnp.sum(weight, axis=1)
    accum = jnp.dot(weight.astype(jnp.bfloat16), band_labels, preferred_element_type=jnp.float32)

    quarter = classes // 4
    core = feat_index % 2
    side = feat_index // 2
    grid = accum.reshape(slots, 2, 2, quarter)
    kept = lax.dynamic_index_in_dim(grid, core, axis=2, keepdims=False)
    sent = lax.dynamic_index_in_dim(grid, 1 - core, axis=2, keepdims=False)
    message = swapped(pack(sent.reshape(slots, 2 * quarter), top, total, 2 * quarter + 12), "feat", 1)
    kept, top, total = merge(kept.reshape(slots, 2 * quarter), top, total, message, 2 * quarter)
    grid = kept.reshape(slots, 2, quarter)
    kept = lax.dynamic_index_in_dim(grid, side, axis=1, keepdims=False)
    sent = lax.dynamic_index_in_dim(grid, 1 - side, axis=1, keepdims=False)
    message = swapped(pack(sent, top, total, quarter + 6), "feat", 2)
    kept, top, total = merge(kept, top, total, message, quarter)
    shares = (kept / total[:, None]).astype(jnp.bfloat16)

    returned = routed(shares.reshape(clusters, capacity, quarter), False)
    return returned.reshape(slots, quarter)[position]


def solution(mesh):
    clusters = mesh.shape["cluster"]
    inner = 8 if clusters % 8 == 0 else 1
    split = Mesh(
        mesh.devices.reshape(clusters // inner, inner, mesh.shape["feat"]), ("outer", "inner", "feat")
    )
    in_specs = (
        P(CLUSTER, "feat"),
        P(CLUSTER, None),
        P(),
        P(CLUSTER + ("feat",), None),
        P(CLUSTER + ("feat",), None),
        P(CLUSTER + ("feat",)),
    )
    out_specs = P(CLUSTER, "feat")
    return jax.shard_map(body, mesh=split, in_specs=in_specs, out_specs=out_specs, check_vma=False)
```

```python
import math

import jax
import jax.numpy as jnp
from jax import lax
from jax.sharding import PartitionSpec as P

REACH = 3


temper = 2.0


def shifted(array, axis, by):
    peers = lax.axis_size(axis)
    return lax.ppermute(array, axis, [(i, (i - by) % peers) for i in range(peers)])


def swapped(array, axis, bit):
    peers = lax.axis_size(axis)
    return lax.ppermute(array, axis, [(i, i ^ bit) for i in range(peers)])


def round_bf16(x):
    return lax.reduce_precision(x, exponent_bits=8, mantissa_bits=7)


def split3(x):
    hi = round_bf16(x)
    rest = x - hi
    mid = round_bf16(rest)
    lo = rest - mid
    return [part.astype(jnp.bfloat16) for part in (hi, mid, lo)]


def join3(parts):
    hi, mid, lo = [p.astype(jnp.float32) for p in parts]
    return (hi + mid) + lo


def pack(part, top, total, width):
    rows = part.shape[0]
    codes = split3(top) + split3(total)
    columns = [part.astype(jnp.bfloat16)] + [c[:, None] for c in codes]
    pad = width - part.shape[1] - len(codes)
    columns.append(jnp.zeros((rows, pad), jnp.bfloat16))
    return jnp.concatenate(columns, axis=1)


def merge(kept, top, total, message, width):
    other = message[:, :width].astype(jnp.float32)
    codes = [message[:, width + i] for i in range(6)]
    other_top = join3(codes[:3])
    other_total = join3(codes[3:])
    highest = jnp.maximum(top, other_top)
    mine = jnp.exp(top - highest)
    theirs = jnp.exp(other_top - highest)
    merged = kept * mine[:, None] + other * theirs[:, None]
    return merged, highest, total * mine + other_total * theirs


def body(queries, assign, band_mask, keys, labels, prior):
    clusters = lax.axis_size("cluster")
    cluster_index = lax.axis_index("cluster")
    feat_index = lax.axis_index("feat")
    feats = lax.axis_size("feat")
    local_rows = queries.shape[0]
    depth = keys.shape[1]
    classes = labels.shape[1]
    rows = keys.shape[0]
    capacity = 2 * local_rows // clusters
    slots = clusters * capacity

    width = depth + classes + 1
    padded = -(-width // 128) * 128
    block = jnp.concatenate(
        [keys, labels, prior[:, None], jnp.zeros((rows, padded - width), keys.dtype)], axis=1
    )
    offsets = [0]
    for reach in range(1, REACH + 1):
        offsets += [reach, -reach]
    blocks = [block] + [shifted(block, "cluster", o) for o in offsets[1:]]

    target = assign[:, 0]
    onehot = (target[:, None] == jnp.arange(clusters, dtype=jnp.int32)[None, :]).astype(jnp.int32)
    before = jnp.cumsum(onehot, axis=0) - onehot
    position = target * capacity + jnp.sum(before * onehot, axis=1)
    outgoing = jnp.zeros((slots, queries.shape[1]), queries.dtype).at[position].set(queries)
    arrived = lax.all_to_all(
        outgoing.reshape(clusters, capacity, queries.shape[1]),
        "cluster",
        split_axis=0,
        concat_axis=0,
        tiled=True,
    )
    own = arrived.reshape(slots, queries.shape[1])
    parts = jnp.stack([own] + [swapped(own, "feat", k) for k in range(1, feats)])
    order = jnp.arange(feats, dtype=jnp.int32) ^ feat_index
    query_full = jnp.swapaxes(jnp.take(parts, order, axis=0), 0, 1).reshape(slots, feats * queries.shape[1])

    stacked = jnp.stack(blocks)
    band_keys = stacked[:, :, :depth].reshape(len(offsets) * rows, depth)
    band_labels = stacked[:, :, depth : depth + classes].reshape(len(offsets) * rows, classes)
    band_prior = stacked[:, :, depth + classes].reshape(len(offsets) * rows)
    mask_row = band_mask[cluster_index]
    live_blocks = jnp.stack([mask_row[REACH + o] > 0 for o in offsets])
    live = jnp.repeat(live_blocks, rows)
    scale = temper / math.sqrt(depth)
    scores = jnp.einsum("qd,kd->qk", query_full, band_keys, preferred_element_type=jnp.float32) * scale
    scores = scores + band_prior.astype(jnp.float32)[None, :]
    scores = jnp.where(live[None, :], scores, -jnp.inf)
    top = jnp.max(scores, axis=1)
    weight = jnp.exp(scores - top[:, None])
    total = jnp.sum(weight, axis=1)
    accum = jnp.dot(weight.astype(jnp.bfloat16), band_labels, preferred_element_type=jnp.float32)

    quarter = classes // feats
    grid = accum.reshape(slots, feats, quarter)
    kept = lax.dynamic_index_in_dim(grid, feat_index, axis=1, keepdims=False)
    messages = [
        swapped(
            pack(lax.dynamic_index_in_dim(grid, feat_index ^ k, axis=1, keepdims=False), top, total, quarter + 6),
            "feat",
            k,
        )
        for k in range(1, feats)
    ]
    for message in messages:
        kept, top, total = merge(kept, top, total, message, quarter)
    shares = (kept / total[:, None]).astype(jnp.bfloat16)

    returned = lax.all_to_all(
        shares.reshape(clusters, capacity, quarter),
        "cluster",
        split_axis=0,
        concat_axis=0,
        tiled=True,
    )
    return returned.reshape(slots, quarter)[position]


def solution(mesh):
    in_specs = (
        P("cluster", "feat"),
        P("cluster", None),
        P(),
        P(("cluster", "feat"), None),
        P(("cluster", "feat"), None),
        P(("cluster", "feat")),
    )
    out_specs = P("cluster", "feat")
    return jax.shard_map(body, mesh=mesh, in_specs=in_specs, out_specs=out_specs, check_vma=False)
```

```python
import math

import jax
import jax.numpy as jnp
from jax import lax
from jax.sharding import PartitionSpec as P

REACH = 3


temper = 2.0


def shifted(array, axis, by):
    peers = lax.axis_size(axis)
    return lax.ppermute(array, axis, [(i, (i - by) % peers) for i in range(peers)])


def swapped(array, axis, bit):
    peers = lax.axis_size(axis)
    return lax.ppermute(array, axis, [(i, i ^ bit) for i in range(peers)])


def round_bf16(x):
    return lax.reduce_precision(x, exponent_bits=8, mantissa_bits=7)


def split3(x):
    hi = round_bf16(x)
    rest = x - hi
    mid = round_bf16(rest)
    lo = rest - mid
    return [part.astype(jnp.bfloat16) for part in (hi, mid, lo)]


def join3(parts):
    hi, mid, lo = [p.astype(jnp.float32) for p in parts]
    return (hi + mid) + lo


def merge(kept, top, total, message, width):
    other = message.astype(jnp.float32)
    other_top = join3([other[:, width + i] for i in range(3)])
    other_total = join3([other[:, width + 3 + i] for i in range(3)])
    highest = jnp.maximum(top, other_top)
    mine = jnp.exp(top - highest)
    theirs = jnp.exp(other_top - highest)
    merged = kept * mine[:, None] + other * theirs[:, None]
    return merged, highest, total * mine + other_total * theirs


def body(queries, assign, band_mask, keys, labels, prior):
    clusters = lax.axis_size("cluster")
    cluster_index = lax.axis_index("cluster")
    feat_index = lax.axis_index("feat")
    feats = lax.axis_size("feat")
    local_rows = queries.shape[0]
    depth = keys.shape[1]
    classes = labels.shape[1]
    rows = keys.shape[0]
    capacity = 2 * local_rows // clusters
    slots = clusters * capacity

    quarter = classes // feats
    group = -(-(quarter + 6) // 128) * 128
    grouped = jnp.pad(labels.reshape(rows, feats, quarter), ((0, 0), (0, 0), (0, group - quarter)))
    grouped = grouped.at[:, 0, quarter].set(prior)
    block = jnp.stack([keys, grouped.reshape(rows, feats * group)])
    offsets = [0]
    for reach in range(1, REACH + 1):
        offsets += [reach, -reach]
    blocks = [block] + [shifted(block, "cluster", o) for o in offsets[1:]]

    target = assign[:, 0]
    onehot = (target[:, None] == jnp.arange(clusters, dtype=jnp.int32)[None, :]).astype(jnp.int32)
    before = jnp.cumsum(onehot, axis=0) - onehot
    position = target * capacity + jnp.sum(before * onehot, axis=1)
    outgoing = jnp.zeros((slots, queries.shape[1]), queries.dtype).at[position].set(queries)
    arrived = lax.all_to_all(
        outgoing.reshape(clusters, capacity, queries.shape[1]),
        "cluster",
        split_axis=0,
        concat_axis=0,
        tiled=True,
    )
    own = arrived.reshape(slots, queries.shape[1])
    parts = jnp.stack([own] + [swapped(own, "feat", k) for k in range(1, feats)])
    order = jnp.arange(feats, dtype=jnp.int32) ^ feat_index
    query_full = jnp.swapaxes(jnp.take(parts, order, axis=0), 0, 1).reshape(slots, feats * queries.shape[1])

    band_keys = jnp.stack([b[0] for b in blocks]).reshape(len(offsets) * rows, depth)
    band_labels = jnp.stack([b[1] for b in blocks]).reshape(len(offsets) * rows, feats * group)
    band_prior = band_labels[:, quarter]
    mask_row = band_mask[cluster_index]
    live_blocks = jnp.stack([mask_row[REACH + o] > 0 for o in offsets])
    live = jnp.repeat(live_blocks, rows)
    scale = temper / math.sqrt(depth)
    scores = jnp.einsum("qd,kd->qk", query_full, band_keys, preferred_element_type=jnp.float32) * scale
    scores = scores + band_prior.astype(jnp.float32)[None, :]
    scores = jnp.where(live[None, :], scores, -jnp.inf)
    top = jnp.max(scores, axis=1)
    weight = jnp.exp(scores - top[:, None])
    total = jnp.sum(weight, axis=1)
    accum = jnp.dot(weight.astype(jnp.bfloat16), band_labels, preferred_element_type=jnp.float32)

    column = lax.broadcasted_iota(jnp.int32, (slots, group), 1)
    codes = split3(top) + split3(total)

    def pack(g):
        part = lax.dynamic_slice_in_dim(accum, g * group, group, axis=1)
        for i, c in enumerate(codes):
            part = jnp.where(column == quarter + i, c.astype(jnp.float32)[:, None], part)
        return part.astype(jnp.bfloat16)

    kept = lax.dynamic_slice_in_dim(accum, feat_index * group, group, axis=1)
    messages = [swapped(pack(feat_index ^ k), "feat", k) for k in range(1, feats)]
    for message in messages:
        kept, top, total = merge(kept, top, total, message, quarter)
    kept = kept[:, :quarter]
    shares = (kept / total[:, None]).astype(jnp.bfloat16)

    returned = lax.all_to_all(
        shares.reshape(clusters, capacity, quarter),
        "cluster",
        split_axis=0,
        concat_axis=0,
        tiled=True,
    )
    return returned.reshape(slots, quarter)[position]


def solution(mesh):
    in_specs = (
        P("cluster", "feat"),
        P("cluster", None),
        P(),
        P(("cluster", "feat"), None),
        P(("cluster", "feat"), None),
        P(("cluster", "feat")),
    )
    out_specs = P("cluster", "feat")
    return jax.shard_map(body, mesh=mesh, in_specs=in_specs, out_specs=out_specs, check_vma=False)
```

```python
import math

import jax
import jax.numpy as jnp
from jax import lax
from jax.sharding import PartitionSpec as P

REACH = 3


temper = 2.0


def shifted(array, axis, by):
    peers = lax.axis_size(axis)
    return lax.ppermute(array, axis, [(i, (i - by) % peers) for i in range(peers)])


def swapped(array, axis, bit):
    peers = lax.axis_size(axis)
    return lax.ppermute(array, axis, [(i, i ^ bit) for i in range(peers)])


def round_bf16(x):
    return lax.reduce_precision(x, exponent_bits=8, mantissa_bits=7)


def split3(x):
    hi = round_bf16(x)
    rest = x - hi
    mid = round_bf16(rest)
    lo = rest - mid
    return [part.astype(jnp.bfloat16) for part in (hi, mid, lo)]


def join3(parts):
    hi, mid, lo = [p.astype(jnp.float32) for p in parts]
    return (hi + mid) + lo


def merge(kept, top, total, message, width):
    other = message.astype(jnp.float32)
    other_top = join3([other[:, width + i] for i in range(3)])
    other_total = join3([other[:, width + 3 + i] for i in range(3)])
    highest = jnp.maximum(top, other_top)
    mine = jnp.exp(top - highest)
    theirs = jnp.exp(other_top - highest)
    merged = kept * mine[:, None] + other * theirs[:, None]
    return merged, highest, total * mine + other_total * theirs


def body(queries, assign, band_mask, keys, labels, prior):
    clusters = lax.axis_size("cluster")
    cluster_index = lax.axis_index("cluster")
    feat_index = lax.axis_index("feat")
    feats = lax.axis_size("feat")
    local_rows = queries.shape[0]
    depth = keys.shape[1]
    classes = labels.shape[1]
    rows = keys.shape[0]
    capacity = 2 * local_rows // clusters
    slots = clusters * capacity

    quarter = classes // feats
    group = -(-(quarter + 6) // 128) * 128
    first = (lax.broadcasted_iota(jnp.int32, (rows, feats, group - quarter), 1) == 0) & (
        lax.broadcasted_iota(jnp.int32, (rows, feats, group - quarter), 2) == 0
    )
    spare = jnp.where(first, prior[:, None, None], jnp.zeros((), prior.dtype))
    grouped = jnp.concatenate([labels.reshape(rows, feats, quarter), spare], axis=2)
    block = jnp.stack([keys, grouped.reshape(rows, feats * group)])
    offsets = [0]
    for reach in range(1, REACH + 1):
        offsets += [reach, -reach]
    blocks = [block] + [shifted(block, "cluster", o) for o in offsets[1:]]

    target = assign[:, 0]
    onehot = (target[:, None] == jnp.arange(clusters, dtype=jnp.int32)[None, :]).astype(jnp.int32)
    before = jnp.cumsum(onehot, axis=0) - onehot
    position = target * capacity + jnp.sum(before * onehot, axis=1)
    outgoing = jnp.zeros((slots, queries.shape[1]), queries.dtype).at[position].set(queries)
    arrived = lax.all_to_all(
        outgoing.reshape(clusters, capacity, queries.shape[1]),
        "cluster",
        split_axis=0,
        concat_axis=0,
        tiled=True,
    )
    own = arrived.reshape(slots, queries.shape[1])
    parts = lax.all_to_all(
        jnp.broadcast_to(own[None], (feats,) + own.shape), "feat", split_axis=0, concat_axis=0, tiled=True
    )
    query_full = jnp.swapaxes(parts, 0, 1).reshape(slots, feats * queries.shape[1])

    band_keys = jnp.stack([b[0] for b in blocks]).reshape(len(offsets) * rows, depth)
    band_labels = jnp.stack([b[1] for b in blocks]).reshape(len(offsets) * rows, feats * group)
    band_prior = band_labels[:, quarter]
    mask_row = band_mask[cluster_index]
    live_blocks = jnp.stack([mask_row[REACH + o] > 0 for o in offsets])
    live = jnp.repeat(live_blocks, rows)
    scale = temper / math.sqrt(depth)
    scores = jnp.einsum("qd,kd->qk", query_full, band_keys, preferred_element_type=jnp.float32) * scale
    scores = scores + band_prior.astype(jnp.float32)[None, :]
    scores = jnp.where(live[None, :], scores, -jnp.inf)
    top = jnp.max(scores, axis=1)
    weight = jnp.exp(scores - top[:, None])
    total = jnp.sum(weight, axis=1)
    accum = jnp.dot(weight.astype(jnp.bfloat16), band_labels, preferred_element_type=jnp.float32)

    column = lax.broadcasted_iota(jnp.int32, (slots, group), 1)
    codes = split3(top) + split3(total)

    def pack(g):
        part = lax.dynamic_slice_in_dim(accum, g * group, group, axis=1)
        for i, c in enumerate(codes):
            part = jnp.where(column == quarter + i, c.astype(jnp.float32)[:, None], part)
        return part.astype(jnp.bfloat16)

    kept = lax.dynamic_slice_in_dim(accum, feat_index * group, group, axis=1)
    outbox = jnp.stack([pack(g) for g in range(feats)])
    inbox = lax.all_to_all(outbox, "feat", split_axis=0, concat_axis=0, tiled=True)
    for k in range(1, feats):
        message = lax.dynamic_index_in_dim(inbox, feat_index ^ k, axis=0, keepdims=False)
        kept, top, total = merge(kept, top, total, message, quarter)
    kept = kept[:, :quarter]
    shares = (kept / total[:, None]).astype(jnp.bfloat16)

    returned = lax.all_to_all(
        shares.reshape(clusters, capacity, quarter),
        "cluster",
        split_axis=0,
        concat_axis=0,
        tiled=True,
    )
    return returned.reshape(slots, quarter)[position]


def solution(mesh):
    in_specs = (
        P("cluster", "feat"),
        P("cluster", None),
        P(),
        P(("cluster", "feat"), None),
        P(("cluster", "feat"), None),
        P(("cluster", "feat")),
    )
    out_specs = P("cluster", "feat")
    return jax.shard_map(body, mesh=mesh, in_specs=in_specs, out_specs=out_specs, check_vma=False)
```

```python
import math

import jax
import jax.numpy as jnp
from jax import lax
from jax.sharding import PartitionSpec as P

REACH = 3


temper = 2.0


def shifted(array, axis, by):
    peers = lax.axis_size(axis)
    return lax.ppermute(array, axis, [(i, (i - by) % peers) for i in range(peers)])


def swapped(array, axis, bit):
    peers = lax.axis_size(axis)
    return lax.ppermute(array, axis, [(i, i ^ bit) for i in range(peers)])


def round_bf16(x):
    return lax.reduce_precision(x, exponent_bits=8, mantissa_bits=7)


def split3(x):
    hi = round_bf16(x)
    rest = x - hi
    mid = round_bf16(rest)
    lo = rest - mid
    return [part.astype(jnp.bfloat16) for part in (hi, mid, lo)]


def join3(parts):
    hi, mid, lo = [p.astype(jnp.float32) for p in parts]
    return (hi + mid) + lo


def merge(kept, top, total, message, width):
    other = message.astype(jnp.float32)
    other_top = join3([other[:, width + i] for i in range(3)])
    other_total = join3([other[:, width + 3 + i] for i in range(3)])
    highest = jnp.maximum(top, other_top)
    mine = jnp.exp(top - highest)
    theirs = jnp.exp(other_top - highest)
    merged = kept * mine[:, None] + other * theirs[:, None]
    return merged, highest, total * mine + other_total * theirs


def body(queries, assign, band_mask, keys, labels, prior):
    clusters = lax.axis_size("cluster")
    cluster_index = lax.axis_index("cluster")
    feat_index = lax.axis_index("feat")
    feats = lax.axis_size("feat")
    local_rows = queries.shape[0]
    depth = keys.shape[1]
    classes = labels.shape[1]
    rows = keys.shape[0]
    capacity = 2 * local_rows // clusters
    slots = clusters * capacity

    quarter = classes // feats
    group = -(-(quarter + 6) // 128) * 128
    first = (lax.broadcasted_iota(jnp.int32, (rows, feats, group - quarter), 1) == 0) & (
        lax.broadcasted_iota(jnp.int32, (rows, feats, group - quarter), 2) == 0
    )
    spare = jnp.where(first, prior[:, None, None], jnp.zeros((), prior.dtype))
    grouped = jnp.concatenate([labels.reshape(rows, feats, quarter), spare], axis=2)
    block = jnp.stack([keys, grouped.reshape(rows, feats * group)])
    offsets = [0]
    for reach in range(1, REACH + 1):
        offsets += [reach, -reach]

    target = assign[:, 0]
    onehot = (target[:, None] == jnp.arange(clusters, dtype=jnp.int32)[None, :]).astype(jnp.int32)
    before = jnp.cumsum(onehot, axis=0) - onehot
    position = target * capacity + jnp.sum(before * onehot, axis=1)
    outgoing = jnp.zeros((slots, queries.shape[1]), queries.dtype).at[position].set(queries)
    arrived = lax.all_to_all(
        outgoing.reshape(clusters, capacity, queries.shape[1]),
        "cluster",
        split_axis=0,
        concat_axis=0,
        tiled=True,
    )
    block, arrived = lax.optimization_barrier((block, arrived))
    blocks = [block] + [shifted(block, "cluster", o) for o in offsets[1:]]
    own = arrived.reshape(slots, queries.shape[1])
    parts = lax.all_to_all(
        jnp.broadcast_to(own[None], (feats,) + own.shape), "feat", split_axis=0, concat_axis=0, tiled=True
    )
    query_full = jnp.swapaxes(parts, 0, 1).reshape(slots, feats * queries.shape[1])

    band_keys = jnp.stack([b[0] for b in blocks]).reshape(len(offsets) * rows, depth)
    band_labels = jnp.stack([b[1] for b in blocks]).reshape(len(offsets) * rows, feats * group)
    band_prior = band_labels[:, quarter]
    mask_row = band_mask[cluster_index]
    live_blocks = jnp.stack([mask_row[REACH + o] > 0 for o in offsets])
    live = jnp.repeat(live_blocks, rows)
    scale = temper / math.sqrt(depth)
    scores = jnp.einsum("qd,kd->qk", query_full, band_keys, preferred_element_type=jnp.float32) * scale
    scores = scores + band_prior.astype(jnp.float32)[None, :]
    scores = jnp.where(live[None, :], scores, -jnp.inf)
    top = jnp.max(scores, axis=1)
    weight = jnp.exp(scores - top[:, None])
    total = jnp.sum(weight, axis=1)
    accum = jnp.dot(weight.astype(jnp.bfloat16), band_labels, preferred_element_type=jnp.float32)

    column = lax.broadcasted_iota(jnp.int32, (slots, group), 1)
    codes = split3(top) + split3(total)

    def pack(g):
        part = lax.dynamic_slice_in_dim(accum, g * group, group, axis=1)
        for i, c in enumerate(codes):
            part = jnp.where(column == quarter + i, c.astype(jnp.float32)[:, None], part)
        return part.astype(jnp.bfloat16)

    kept = lax.dynamic_slice_in_dim(accum, feat_index * group, group, axis=1)
    outbox = jnp.stack([pack(g) for g in range(feats)])
    inbox = lax.all_to_all(outbox, "feat", split_axis=0, concat_axis=0, tiled=True)
    for k in range(1, feats):
        message = lax.dynamic_index_in_dim(inbox, feat_index ^ k, axis=0, keepdims=False)
        kept, top, total = merge(kept, top, total, message, quarter)
    kept = kept[:, :quarter]
    shares = (kept / total[:, None]).astype(jnp.bfloat16)

    returned = lax.all_to_all(
        shares.reshape(clusters, capacity, quarter),
        "cluster",
        split_axis=0,
        concat_axis=0,
        tiled=True,
    )
    return returned.reshape(slots, quarter)[position]


def solution(mesh):
    in_specs = (
        P("cluster", "feat"),
        P("cluster", None),
        P(),
        P(("cluster", "feat"), None),
        P(("cluster", "feat"), None),
        P(("cluster", "feat")),
    )
    out_specs = P("cluster", "feat")
    return jax.shard_map(body, mesh=mesh, in_specs=in_specs, out_specs=out_specs, check_vma=False)
```

```python
import math

import jax
import jax.numpy as jnp
from jax import lax
from jax.sharding import PartitionSpec as P

REACH = 3


temper = 2.0


def shifted(array, axis, by):
    peers = lax.axis_size(axis)
    return lax.ppermute(array, axis, [(i, (i - by) % peers) for i in range(peers)])


def swapped(array, axis, bit):
    peers = lax.axis_size(axis)
    return lax.ppermute(array, axis, [(i, i ^ bit) for i in range(peers)])


def round_bf16(x):
    return lax.reduce_precision(x, exponent_bits=8, mantissa_bits=7)


def split3(x):
    hi = round_bf16(x)
    rest = x - hi
    mid = round_bf16(rest)
    lo = rest - mid
    return [part.astype(jnp.bfloat16) for part in (hi, mid, lo)]


def join3(parts):
    hi, mid, lo = [p.astype(jnp.float32) for p in parts]
    return (hi + mid) + lo


def merge(kept, top, total, message, width):
    other = message.astype(jnp.float32)
    other_top = join3([other[:, width + i] for i in range(3)])
    other_total = join3([other[:, width + 3 + i] for i in range(3)])
    highest = jnp.maximum(top, other_top)
    mine = jnp.exp(top - highest)
    theirs = jnp.exp(other_top - highest)
    merged = kept * mine[:, None] + other * theirs[:, None]
    return merged, highest, total * mine + other_total * theirs


def body(queries, assign, band_mask, keys, labels, prior):
    clusters = lax.axis_size("cluster")
    cluster_index = lax.axis_index("cluster")
    feat_index = lax.axis_index("feat")
    feats = lax.axis_size("feat")
    local_rows = queries.shape[0]
    depth = keys.shape[1]
    classes = labels.shape[1]
    rows = keys.shape[0]
    capacity = 2 * local_rows // clusters
    slots = clusters * capacity

    quarter = classes // feats
    group = -(-(quarter + 6) // 128) * 128
    first = (lax.broadcasted_iota(jnp.int32, (rows, feats, group - quarter), 1) == 0) & (
        lax.broadcasted_iota(jnp.int32, (rows, feats, group - quarter), 2) == 0
    )
    spare = jnp.where(first, prior[:, None, None], jnp.zeros((), prior.dtype))
    grouped = jnp.concatenate([labels.reshape(rows, feats, quarter), spare], axis=2)
    block = jnp.stack([keys, grouped.reshape(rows, feats * group)])
    offsets = [0]
    for reach in range(1, REACH + 1):
        offsets += [reach, -reach]
    blocks = [block] + [shifted(block, "cluster", o) for o in offsets[1:]]

    target = assign[:, 0]
    onehot = (target[:, None] == jnp.arange(clusters, dtype=jnp.int32)[None, :]).astype(jnp.int32)
    before = jnp.cumsum(onehot, axis=0) - onehot
    position = target * capacity + jnp.sum(before * onehot, axis=1)
    outgoing = jnp.zeros((slots, queries.shape[1]), queries.dtype).at[position].set(queries)
    arrived = lax.all_to_all(
        outgoing.reshape(clusters, capacity, queries.shape[1]),
        "cluster",
        split_axis=0,
        concat_axis=0,
        tiled=True,
    )
    own = arrived.reshape(slots, queries.shape[1])
    far = swapped(own, "feat", 2)
    near = swapped(jnp.stack([own, far]), "feat", 1)
    parts = jnp.stack([own, far, near[0], near[1]])
    order = jnp.array([0, 2, 1, 3], jnp.int32)[jnp.arange(feats, dtype=jnp.int32) ^ feat_index]
    query_full = jnp.swapaxes(jnp.take(parts, order, axis=0), 0, 1).reshape(slots, feats * queries.shape[1])

    band_keys = jnp.stack([b[0] for b in blocks]).reshape(len(offsets) * rows, depth)
    band_labels = jnp.stack([b[1] for b in blocks]).reshape(len(offsets) * rows, feats * group)
    band_prior = band_labels[:, quarter]
    mask_row = band_mask[cluster_index]
    live_blocks = jnp.stack([mask_row[REACH + o] > 0 for o in offsets])
    live = jnp.repeat(live_blocks, rows)
    scale = temper / math.sqrt(depth)
    scores = jnp.einsum("qd,kd->qk", query_full, band_keys, preferred_element_type=jnp.float32) * scale
    scores = scores + band_prior.astype(jnp.float32)[None, :]
    scores = jnp.where(live[None, :], scores, -jnp.inf)
    top = jnp.max(scores, axis=1)
    weight = jnp.exp(scores - top[:, None])
    total = jnp.sum(weight, axis=1)
    accum = jnp.dot(weight.astype(jnp.bfloat16), band_labels, preferred_element_type=jnp.float32)

    column = lax.broadcasted_iota(jnp.int32, (slots, group), 1)

    def pack(part, top, total):
        for i, c in enumerate(split3(top) + split3(total)):
            part = jnp.where(column == quarter + i, c.astype(jnp.float32)[:, None], part)
        return part.astype(jnp.bfloat16)

    grid = accum.reshape(slots, feats, group)
    pick = lambda g: lax.dynamic_index_in_dim(grid, g, axis=1, keepdims=False)
    kept = jnp.stack([pick(feat_index), pick(feat_index ^ 2)])
    sent = jnp.stack([pack(pick(feat_index ^ 1), top, total), pack(pick(feat_index ^ 3), top, total)])
    message = swapped(sent, "feat", 1).astype(jnp.float32)
    other_top = join3([message[0, :, quarter + i] for i in range(3)])
    other_total = join3([message[0, :, quarter + 3 + i] for i in range(3)])
    highest = jnp.maximum(top, other_top)
    mine = jnp.exp(top - highest)
    theirs = jnp.exp(other_top - highest)
    kept = kept * mine[None, :, None] + message * theirs[None, :, None]
    top, total = highest, total * mine + other_total * theirs
    message = swapped(pack(kept[1], top, total), "feat", 2)
    kept, top, total = merge(kept[0], top, total, message, quarter)
    kept = kept[:, :quarter]
    shares = (kept / total[:, None]).astype(jnp.bfloat16)

    returned = lax.all_to_all(
        shares.reshape(clusters, capacity, quarter),
        "cluster",
        split_axis=0,
        concat_axis=0,
        tiled=True,
    )
    return returned.reshape(slots, quarter)[position]


def solution(mesh):
    in_specs = (
        P("cluster", "feat"),
        P("cluster", None),
        P(),
        P(("cluster", "feat"), None),
        P(("cluster", "feat"), None),
        P(("cluster", "feat")),
    )
    out_specs = P("cluster", "feat")
    return jax.shard_map(body, mesh=mesh, in_specs=in_specs, out_specs=out_specs, check_vma=False)
```

```python
import functools
import math

import jax
import jax.numpy as jnp
from jax import lax
from jax.experimental import pallas as pl
from jax.experimental.pallas import tpu as pltpu
from jax.sharding import PartitionSpec as P

REACH = 3


temper = 2.0


def shifted(array, axis, by):
    peers = lax.axis_size(axis)
    return lax.ppermute(array, axis, [(i, (i - by) % peers) for i in range(peers)])


def swapped(array, axis, bit):
    peers = lax.axis_size(axis)
    return lax.ppermute(array, axis, [(i, i ^ bit) for i in range(peers)])


def round_bf16(x):
    return lax.reduce_precision(x, exponent_bits=8, mantissa_bits=7)


def split3(x):
    hi = round_bf16(x)
    rest = x - hi
    mid = round_bf16(rest)
    lo = rest - mid
    return [part.astype(jnp.bfloat16) for part in (hi, mid, lo)]


def join3(parts):
    hi, mid, lo = [p.astype(jnp.float32) for p in parts]
    return (hi + mid) + lo


def merge(kept, top, total, message, width):
    other = message.astype(jnp.float32)
    other_top = join3([other[:, width + i] for i in range(3)])
    other_total = join3([other[:, width + 3 + i] for i in range(3)])
    highest = jnp.maximum(top, other_top)
    mine = jnp.exp(top - highest)
    theirs = jnp.exp(other_top - highest)
    merged = kept * mine[:, None] + other * theirs[:, None]
    return merged, highest, total * mine + other_total * theirs


def band_kernel(scale, count, query_ref, row_ref, *refs):
    blocks = refs[:count]
    accum_ref, top_ref, total_ref, score_ref, weight_ref = refs[count:]
    rows = blocks[0].shape[1]
    query = query_ref[...]
    for b in range(count):
        cut = slice(b * rows, (b + 1) * rows)
        part = lax.dot_general(
            query, blocks[b][0], (((1,), (1,)), ((), ())), preferred_element_type=jnp.float32
        )
        score_ref[:, cut] = part * scale + row_ref[:, cut]
    scores = score_ref[...]
    top = jnp.max(scores, axis=1, keepdims=True)
    weight = jnp.exp(scores - top)
    total = jnp.sum(weight, axis=1, keepdims=True)
    weight_ref[...] = weight.astype(jnp.bfloat16)
    top_ref[...] = jnp.broadcast_to(top, top_ref.shape)
    total_ref[...] = jnp.broadcast_to(total, total_ref.shape)
    accum = jnp.zeros(accum_ref.shape, jnp.float32)
    for b in range(count):
        cut = slice(b * rows, (b + 1) * rows)
        accum = accum + jnp.dot(weight_ref[:, cut], blocks[b][1], preferred_element_type=jnp.float32)
    accum_ref[...] = accum


def band(query_full, row, blocks, scale):
    slots, depth = query_full.shape
    count = len(blocks)
    rows, width = blocks[0].shape[1], blocks[0].shape[2]
    band_rows = count * rows
    out_shape = [
        jax.ShapeDtypeStruct((slots, width), jnp.float32),
        jax.ShapeDtypeStruct((slots, 128), jnp.float32),
        jax.ShapeDtypeStruct((slots, 128), jnp.float32),
    ]
    cost = pl.CostEstimate(
        flops=2 * slots * band_rows * (depth + width),
        transcendentals=slots * band_rows,
        bytes_accessed=2 * slots * depth + 2 * band_rows * (depth + width) + 4 * slots * width,
    )
    accum, top, total = pl.pallas_call(
        functools.partial(band_kernel, scale, count),
        out_shape=out_shape,
        scratch_shapes=[
            pltpu.VMEM((slots, band_rows), jnp.float32),
            pltpu.VMEM((slots, band_rows), jnp.bfloat16),
        ],
        cost_estimate=cost,
    )(query_full, row, *blocks)
    return accum, top[:, 0], total[:, 0]


def body(queries, assign, band_mask, keys, labels, prior):
    clusters = lax.axis_size("cluster")
    cluster_index = lax.axis_index("cluster")
    feat_index = lax.axis_index("feat")
    feats = lax.axis_size("feat")
    local_rows = queries.shape[0]
    depth = keys.shape[1]
    classes = labels.shape[1]
    rows = keys.shape[0]
    capacity = 2 * local_rows // clusters
    slots = clusters * capacity

    quarter = classes // feats
    group = -(-(quarter + 6) // 128) * 128
    first = (lax.broadcasted_iota(jnp.int32, (rows, feats, group - quarter), 1) == 0) & (
        lax.broadcasted_iota(jnp.int32, (rows, feats, group - quarter), 2) == 0
    )
    spare = jnp.where(first, prior[:, None, None], jnp.zeros((), prior.dtype))
    grouped = jnp.concatenate([labels.reshape(rows, feats, quarter), spare], axis=2)
    block = jnp.stack([keys, grouped.reshape(rows, feats * group)])
    offsets = [0]
    for reach in range(1, REACH + 1):
        offsets += [reach, -reach]
    blocks = [block] + [shifted(block, "cluster", o) for o in offsets[1:]]

    target = assign[:, 0]
    onehot = (target[:, None] == jnp.arange(clusters, dtype=jnp.int32)[None, :]).astype(jnp.int32)
    before = jnp.cumsum(onehot, axis=0) - onehot
    position = target * capacity + jnp.sum(before * onehot, axis=1)
    outgoing = jnp.zeros((slots, queries.shape[1]), queries.dtype).at[position].set(queries)
    arrived = lax.all_to_all(
        outgoing.reshape(clusters, capacity, queries.shape[1]),
        "cluster",
        split_axis=0,
        concat_axis=0,
        tiled=True,
    )
    own = arrived.reshape(slots, queries.shape[1])
    far = swapped(own, "feat", 2)
    near = swapped(jnp.stack([own, far]), "feat", 1)
    parts = jnp.stack([own, far, near[0], near[1]])
    order = jnp.array([0, 2, 1, 3], jnp.int32)[jnp.arange(feats, dtype=jnp.int32) ^ feat_index]
    query_full = jnp.swapaxes(jnp.take(parts, order, axis=0), 0, 1).reshape(slots, feats * queries.shape[1])

    mask_row = band_mask[cluster_index]
    live_blocks = jnp.stack([mask_row[REACH + o] > 0 for o in offsets])
    live = jnp.repeat(live_blocks, rows)
    band_prior = jnp.concatenate([b[1][:, quarter] for b in blocks]).astype(jnp.float32)
    row = jnp.where(live, band_prior, -jnp.inf)[None, :]
    scale = temper / math.sqrt(depth)
    accum, top, total = band(query_full, row, blocks, scale)

    column = lax.broadcasted_iota(jnp.int32, (slots, group), 1)

    def pack(part, top, total):
        for i, c in enumerate(split3(top) + split3(total)):
            part = jnp.where(column == quarter + i, c.astype(jnp.float32)[:, None], part)
        return part.astype(jnp.bfloat16)

    grid = accum.reshape(slots, feats, group)
    pick = lambda g: lax.dynamic_index_in_dim(grid, g, axis=1, keepdims=False)
    kept = jnp.stack([pick(feat_index), pick(feat_index ^ 2)])
    sent = jnp.stack([pack(pick(feat_index ^ 1), top, total), pack(pick(feat_index ^ 3), top, total)])
    message = swapped(sent, "feat", 1).astype(jnp.float32)
    other_top = join3([message[0, :, quarter + i] for i in range(3)])
    other_total = join3([message[0, :, quarter + 3 + i] for i in range(3)])
    highest = jnp.maximum(top, other_top)
    mine = jnp.exp(top - highest)
    theirs = jnp.exp(other_top - highest)
    kept = kept * mine[None, :, None] + message * theirs[None, :, None]
    top, total = highest, total * mine + other_total * theirs
    message = swapped(pack(kept[1], top, total), "feat", 2)
    kept, top, total = merge(kept[0], top, total, message, quarter)
    kept = kept[:, :quarter]
    shares = (kept / total[:, None]).astype(jnp.bfloat16)

    returned = lax.all_to_all(
        shares.reshape(clusters, capacity, quarter),
        "cluster",
        split_axis=0,
        concat_axis=0,
        tiled=True,
    )
    return returned.reshape(slots, quarter)[position]


def solution(mesh):
    in_specs = (
        P("cluster", "feat"),
        P("cluster", None),
        P(),
        P(("cluster", "feat"), None),
        P(("cluster", "feat"), None),
        P(("cluster", "feat")),
    )
    out_specs = P("cluster", "feat")
    return jax.shard_map(body, mesh=mesh, in_specs=in_specs, out_specs=out_specs, check_vma=False)
```

```python
import functools
import math

import jax
import jax.numpy as jnp
from jax import lax
from jax.experimental import pallas as pl
from jax.experimental.pallas import tpu as pltpu
from jax.sharding import PartitionSpec as P

REACH = 3


temper = 2.0


def shifted(array, axis, by):
    peers = lax.axis_size(axis)
    return lax.ppermute(array, axis, [(i, (i - by) % peers) for i in range(peers)])


def swapped(array, axis, bit):
    peers = lax.axis_size(axis)
    return lax.ppermute(array, axis, [(i, i ^ bit) for i in range(peers)])


def round_bf16(x):
    return lax.reduce_precision(x, exponent_bits=8, mantissa_bits=7)


def split3(x):
    hi = round_bf16(x)
    rest = x - hi
    mid = round_bf16(rest)
    lo = rest - mid
    return [part.astype(jnp.bfloat16) for part in (hi, mid, lo)]


def join3(parts):
    hi, mid, lo = [p.astype(jnp.float32) for p in parts]
    return (hi + mid) + lo


def merge(kept, top, total, message, width):
    other = message.astype(jnp.float32)
    other_top = join3([other[:, width + i] for i in range(3)])
    other_total = join3([other[:, width + 3 + i] for i in range(3)])
    highest = jnp.maximum(top, other_top)
    mine = jnp.exp(top - highest)
    theirs = jnp.exp(other_top - highest)
    merged = kept * mine[:, None] + other * theirs[:, None]
    return merged, highest, total * mine + other_total * theirs


def band_kernel(scale, count, query_ref, row_ref, *refs):
    blocks = refs[:count]
    accum_ref, top_ref, total_ref, score_ref, weight_ref = refs[count:]
    rows = blocks[0].shape[1]
    query = query_ref[...]
    for b in range(count):
        cut = slice(b * rows, (b + 1) * rows)
        part = lax.dot_general(
            query, blocks[b][0], (((1,), (1,)), ((), ())), preferred_element_type=jnp.float32
        )
        score_ref[:, cut] = part * scale + row_ref[:, cut]
    scores = score_ref[...]
    top = jnp.max(scores, axis=1, keepdims=True)
    weight = jnp.exp(scores - top)
    total = jnp.sum(weight, axis=1, keepdims=True)
    weight_ref[...] = weight.astype(jnp.bfloat16)
    top_ref[...] = jnp.broadcast_to(top, top_ref.shape)
    total_ref[...] = jnp.broadcast_to(total, total_ref.shape)
    accum_ref[...] = jnp.dot(weight_ref[:, :rows], blocks[0][1], preferred_element_type=jnp.float32)
    for b in range(1, count):
        cut = slice(b * rows, (b + 1) * rows)
        accum_ref[...] += jnp.dot(weight_ref[:, cut], blocks[b][1], preferred_element_type=jnp.float32)


def band(query_full, row, blocks, scale, tile=128):
    slots, depth = query_full.shape
    count = len(blocks)
    rows, width = blocks[0].shape[1], blocks[0].shape[2]
    band_rows = count * rows
    out_shape = [
        jax.ShapeDtypeStruct((slots, width), jnp.float32),
        jax.ShapeDtypeStruct((slots, 128), jnp.float32),
        jax.ShapeDtypeStruct((slots, 128), jnp.float32),
    ]
    cost = pl.CostEstimate(
        flops=2 * slots * band_rows * (depth + width),
        transcendentals=slots * band_rows,
        bytes_accessed=2 * slots * depth + 2 * band_rows * (depth + width) + 4 * slots * width,
    )
    whole = pl.BlockSpec(blocks[0].shape, lambda i: (0, 0, 0))
    accum, top, total = pl.pallas_call(
        functools.partial(band_kernel, scale, count),
        out_shape=out_shape,
        grid=(slots // tile,),
        in_specs=[
            pl.BlockSpec((tile, depth), lambda i: (i, 0)),
            pl.BlockSpec((1, band_rows), lambda i: (0, 0)),
        ]
        + [whole] * count,
        out_specs=[
            pl.BlockSpec((tile, width), lambda i: (i, 0)),
            pl.BlockSpec((tile, 128), lambda i: (i, 0)),
            pl.BlockSpec((tile, 128), lambda i: (i, 0)),
        ],
        scratch_shapes=[
            pltpu.VMEM((tile, band_rows), jnp.float32),
            pltpu.VMEM((tile, band_rows), jnp.bfloat16),
        ],
        cost_estimate=cost,
    )(query_full, row, *blocks)
    return accum, top[:, 0], total[:, 0]


def body(queries, assign, band_mask, keys, labels, prior):
    clusters = lax.axis_size("cluster")
    cluster_index = lax.axis_index("cluster")
    feat_index = lax.axis_index("feat")
    feats = lax.axis_size("feat")
    local_rows = queries.shape[0]
    depth = keys.shape[1]
    classes = labels.shape[1]
    rows = keys.shape[0]
    capacity = 2 * local_rows // clusters
    slots = clusters * capacity

    quarter = classes // feats
    group = -(-(quarter + 6) // 128) * 128
    first = (lax.broadcasted_iota(jnp.int32, (rows, feats, group - quarter), 1) == 0) & (
        lax.broadcasted_iota(jnp.int32, (rows, feats, group - quarter), 2) == 0
    )
    spare = jnp.where(first, prior[:, None, None], jnp.zeros((), prior.dtype))
    grouped = jnp.concatenate([labels.reshape(rows, feats, quarter), spare], axis=2)
    block = jnp.stack([keys, grouped.reshape(rows, feats * group)])
    offsets = [0]
    for reach in range(1, REACH + 1):
        offsets += [reach, -reach]
    blocks = [block] + [shifted(block, "cluster", o) for o in offsets[1:]]

    target = assign[:, 0]
    onehot = (target[:, None] == jnp.arange(clusters, dtype=jnp.int32)[None, :]).astype(jnp.int32)
    before = jnp.cumsum(onehot, axis=0) - onehot
    position = target * capacity + jnp.sum(before * onehot, axis=1)
    outgoing = jnp.zeros((slots, queries.shape[1]), queries.dtype).at[position].set(queries)
    arrived = lax.all_to_all(
        outgoing.reshape(clusters, capacity, queries.shape[1]),
        "cluster",
        split_axis=0,
        concat_axis=0,
        tiled=True,
    )
    own = arrived.reshape(slots, queries.shape[1])
    far = swapped(own, "feat", 2)
    near = swapped(jnp.stack([own, far]), "feat", 1)
    parts = jnp.stack([own, far, near[0], near[1]])
    order = jnp.array([0, 2, 1, 3], jnp.int32)[jnp.arange(feats, dtype=jnp.int32) ^ feat_index]
    query_full = jnp.swapaxes(jnp.take(parts, order, axis=0), 0, 1).reshape(slots, feats * queries.shape[1])

    mask_row = band_mask[cluster_index]
    live_blocks = jnp.stack([mask_row[REACH + o] > 0 for o in offsets])
    live = jnp.repeat(live_blocks, rows)
    band_prior = jnp.concatenate([b[1][:, quarter] for b in blocks]).astype(jnp.float32)
    row = jnp.where(live, band_prior, -jnp.inf)[None, :]
    scale = temper / math.sqrt(depth)
    accum, top, total = band(query_full, row, blocks, scale)

    column = lax.broadcasted_iota(jnp.int32, (slots, group), 1)

    def pack(part, top, total):
        for i, c in enumerate(split3(top) + split3(total)):
            part = jnp.where(column == quarter + i, c.astype(jnp.float32)[:, None], part)
        return part.astype(jnp.bfloat16)

    grid = accum.reshape(slots, feats, group)
    pick = lambda g: lax.dynamic_index_in_dim(grid, g, axis=1, keepdims=False)
    kept = jnp.stack([pick(feat_index), pick(feat_index ^ 2)])
    sent = jnp.stack([pack(pick(feat_index ^ 1), top, total), pack(pick(feat_index ^ 3), top, total)])
    message = swapped(sent, "feat", 1).astype(jnp.float32)
    other_top = join3([message[0, :, quarter + i] for i in range(3)])
    other_total = join3([message[0, :, quarter + 3 + i] for i in range(3)])
    highest = jnp.maximum(top, other_top)
    mine = jnp.exp(top - highest)
    theirs = jnp.exp(other_top - highest)
    kept = kept * mine[None, :, None] + message * theirs[None, :, None]
    top, total = highest, total * mine + other_total * theirs
    message = swapped(pack(kept[1], top, total), "feat", 2)
    kept, top, total = merge(kept[0], top, total, message, quarter)
    kept = kept[:, :quarter]
    shares = (kept / total[:, None]).astype(jnp.bfloat16)

    returned = lax.all_to_all(
        shares.reshape(clusters, capacity, quarter),
        "cluster",
        split_axis=0,
        concat_axis=0,
        tiled=True,
    )
    return returned.reshape(slots, quarter)[position]


def solution(mesh):
    in_specs = (
        P("cluster", "feat"),
        P("cluster", None),
        P(),
        P(("cluster", "feat"), None),
        P(("cluster", "feat"), None),
        P(("cluster", "feat")),
    )
    out_specs = P("cluster", "feat")
    return jax.shard_map(body, mesh=mesh, in_specs=in_specs, out_specs=out_specs, check_vma=False)
```

```python
import math

import jax
import jax.numpy as jnp
from jax import lax
from jax.sharding import PartitionSpec as P

REACH = 3


temper = 2.0


def shifted(array, axis, by):
    peers = lax.axis_size(axis)
    return lax.ppermute(array, axis, [(i, (i - by) % peers) for i in range(peers)])


def swapped(array, axis, bit):
    peers = lax.axis_size(axis)
    return lax.ppermute(array, axis, [(i, i ^ bit) for i in range(peers)])


def round_bf16(x):
    return lax.reduce_precision(x, exponent_bits=8, mantissa_bits=7)


def split3(x):
    hi = round_bf16(x)
    rest = x - hi
    mid = round_bf16(rest)
    lo = rest - mid
    return [part.astype(jnp.bfloat16) for part in (hi, mid, lo)]


def join3(parts):
    hi, mid, lo = [p.astype(jnp.float32) for p in parts]
    return (hi + mid) + lo


def merge(kept, top, total, message, width):
    other = message.astype(jnp.float32)
    other_top = join3([other[:, width + i] for i in range(3)])
    other_total = join3([other[:, width + 3 + i] for i in range(3)])
    highest = jnp.maximum(top, other_top)
    mine = jnp.exp(top - highest)
    theirs = jnp.exp(other_top - highest)
    merged = kept * mine[:, None] + other * theirs[:, None]
    return merged, highest, total * mine + other_total * theirs


def body(queries, assign, band_mask, keys, labels, prior):
    clusters = lax.axis_size("cluster")
    cluster_index = lax.axis_index("cluster")
    feat_index = lax.axis_index("feat")
    feats = lax.axis_size("feat")
    local_rows = queries.shape[0]
    depth = keys.shape[1]
    classes = labels.shape[1]
    rows = keys.shape[0]
    capacity = 2 * local_rows // clusters
    slots = clusters * capacity

    quarter = classes // feats
    group = -(-(quarter + 6) // 128) * 128
    first = (lax.broadcasted_iota(jnp.int32, (rows, feats, group - quarter), 1) == 0) & (
        lax.broadcasted_iota(jnp.int32, (rows, feats, group - quarter), 2) == 0
    )
    spare = jnp.where(first, prior[:, None, None], jnp.zeros((), prior.dtype))
    grouped = jnp.concatenate([labels.reshape(rows, feats, quarter), spare], axis=2)
    block = jnp.stack([keys, grouped.reshape(rows, feats * group)])
    offsets = [0]
    for reach in range(1, REACH + 1):
        offsets += [reach, -reach]
    above = shifted(block, "cluster", 1)
    below = shifted(block, "cluster", -1)
    pair = jnp.stack([block, above])
    far_above = shifted(pair, "cluster", 2)
    far_below = shifted(pair, "cluster", -3)
    reached = {0: block, 1: above, -1: below, 2: far_above[0], 3: far_above[1], -3: far_below[0], -2: far_below[1]}
    blocks = [reached[o] for o in offsets]

    target = assign[:, 0]
    onehot = (target[:, None] == jnp.arange(clusters, dtype=jnp.int32)[None, :]).astype(jnp.int32)
    before = jnp.cumsum(onehot, axis=0) - onehot
    position = target * capacity + jnp.sum(before * onehot, axis=1)
    outgoing = jnp.zeros((slots, queries.shape[1]), queries.dtype).at[position].set(queries)
    arrived = lax.all_to_all(
        outgoing.reshape(clusters, capacity, queries.shape[1]),
        "cluster",
        split_axis=0,
        concat_axis=0,
        tiled=True,
    )
    own = arrived.reshape(slots, queries.shape[1])
    far = swapped(own, "feat", 2)
    near = swapped(jnp.stack([own, far]), "feat", 1)
    parts = jnp.stack([own, far, near[0], near[1]])
    order = jnp.array([0, 2, 1, 3], jnp.int32)[jnp.arange(feats, dtype=jnp.int32) ^ feat_index]
    query_full = jnp.swapaxes(jnp.take(parts, order, axis=0), 0, 1).reshape(slots, feats * queries.shape[1])

    band_keys = jnp.stack([b[0] for b in blocks]).reshape(len(offsets) * rows, depth)
    band_labels = jnp.stack([b[1] for b in blocks]).reshape(len(offsets) * rows, feats * group)
    band_prior = band_labels[:, quarter]
    mask_row = band_mask[cluster_index]
    live_blocks = jnp.stack([mask_row[REACH + o] > 0 for o in offsets])
    live = jnp.repeat(live_blocks, rows)
    scale = temper / math.sqrt(depth)
    scores = jnp.einsum("qd,kd->qk", query_full, band_keys, preferred_element_type=jnp.float32) * scale
    scores = scores + band_prior.astype(jnp.float32)[None, :]
    scores = jnp.where(live[None, :], scores, -jnp.inf)
    top = jnp.max(scores, axis=1)
    weight = jnp.exp(scores - top[:, None])
    total = jnp.sum(weight, axis=1)
    accum = jnp.dot(weight.astype(jnp.bfloat16), band_labels, preferred_element_type=jnp.float32)

    column = lax.broadcasted_iota(jnp.int32, (slots, group), 1)

    def pack(part, top, total):
        for i, c in enumerate(split3(top) + split3(total)):
            part = jnp.where(column == quarter + i, c.astype(jnp.float32)[:, None], part)
        return part.astype(jnp.bfloat16)

    grid = accum.reshape(slots, feats, group)
    pick = lambda g: lax.dynamic_index_in_dim(grid, g, axis=1, keepdims=False)
    kept = jnp.stack([pick(feat_index), pick(feat_index ^ 2)])
    sent = jnp.stack([pack(pick(feat_index ^ 1), top, total), pack(pick(feat_index ^ 3), top, total)])
    message = swapped(sent, "feat", 1).astype(jnp.float32)
    other_top = join3([message[0, :, quarter + i] for i in range(3)])
    other_total = join3([message[0, :, quarter + 3 + i] for i in range(3)])
    highest = jnp.maximum(top, other_top)
    mine = jnp.exp(top - highest)
    theirs = jnp.exp(other_top - highest)
    kept = kept * mine[None, :, None] + message * theirs[None, :, None]
    top, total = highest, total * mine + other_total * theirs
    message = swapped(pack(kept[1], top, total), "feat", 2)
    kept, top, total = merge(kept[0], top, total, message, quarter)
    kept = kept[:, :quarter]
    shares = (kept / total[:, None]).astype(jnp.bfloat16)

    returned = lax.all_to_all(
        shares.reshape(clusters, capacity, quarter),
        "cluster",
        split_axis=0,
        concat_axis=0,
        tiled=True,
    )
    return returned.reshape(slots, quarter)[position]


def solution(mesh):
    in_specs = (
        P("cluster", "feat"),
        P("cluster", None),
        P(),
        P(("cluster", "feat"), None),
        P(("cluster", "feat"), None),
        P(("cluster", "feat")),
    )
    out_specs = P("cluster", "feat")
    return jax.shard_map(body, mesh=mesh, in_specs=in_specs, out_specs=out_specs, check_vma=False)
```

```python
import math

import jax
import jax.numpy as jnp
from jax import lax
from jax.sharding import PartitionSpec as P

REACH = 3


temper = 2.0


def shifted(array, axis, by):
    peers = lax.axis_size(axis)
    return lax.ppermute(array, axis, [(i, (i - by) % peers) for i in range(peers)])


def swapped(array, axis, bit):
    peers = lax.axis_size(axis)
    return lax.ppermute(array, axis, [(i, i ^ bit) for i in range(peers)])


def round_bf16(x):
    return lax.reduce_precision(x, exponent_bits=8, mantissa_bits=7)


def split3(x):
    hi = round_bf16(x)
    rest = x - hi
    mid = round_bf16(rest)
    lo = rest - mid
    return [part.astype(jnp.bfloat16) for part in (hi, mid, lo)]


def join3(parts):
    hi, mid, lo = [p.astype(jnp.float32) for p in parts]
    return (hi + mid) + lo


def merge(kept, top, total, message, width):
    other = message.astype(jnp.float32)
    other_top = join3([other[:, width + i] for i in range(3)])
    other_total = join3([other[:, width + 3 + i] for i in range(3)])
    highest = jnp.maximum(top, other_top)
    mine = jnp.exp(top - highest)
    theirs = jnp.exp(other_top - highest)
    merged = kept * mine[:, None] + other * theirs[:, None]
    return merged, highest, total * mine + other_total * theirs


def body(queries, assign, band_mask, keys, labels, prior):
    clusters = lax.axis_size("cluster")
    cluster_index = lax.axis_index("cluster")
    feat_index = lax.axis_index("feat")
    feats = lax.axis_size("feat")
    local_rows = queries.shape[0]
    depth = keys.shape[1]
    classes = labels.shape[1]
    rows = keys.shape[0]
    capacity = 2 * local_rows // clusters
    slots = clusters * capacity

    quarter = classes // feats
    group = -(-(quarter + 6) // 128) * 128
    first = (lax.broadcasted_iota(jnp.int32, (rows, feats, group - quarter), 1) == 0) & (
        lax.broadcasted_iota(jnp.int32, (rows, feats, group - quarter), 2) == 0
    )
    spare = jnp.where(first, prior[:, None, None], jnp.zeros((), prior.dtype))
    grouped = jnp.concatenate([labels.reshape(rows, feats, quarter), spare], axis=2)
    block = jnp.stack([keys, grouped.reshape(rows, feats * group)])
    offsets = [0]
    for reach in range(1, REACH + 1):
        offsets += [reach, -reach]
    blocks = [block] + [shifted(block, "cluster", o) for o in offsets[1:]]

    target = assign[:, 0]
    onehot = (target[:, None] == jnp.arange(clusters, dtype=jnp.int32)[None, :]).astype(jnp.int32)
    before = jnp.cumsum(onehot, axis=0) - onehot
    position = target * capacity + jnp.sum(before * onehot, axis=1)
    placed = (lax.broadcasted_iota(jnp.int32, (slots, local_rows), 0) == position[None, :]).astype(queries.dtype)
    outgoing = jnp.dot(placed, queries, preferred_element_type=jnp.float32).astype(queries.dtype)
    arrived = lax.all_to_all(
        outgoing.reshape(clusters, capacity, queries.shape[1]),
        "cluster",
        split_axis=0,
        concat_axis=0,
        tiled=True,
    )
    own = arrived.reshape(slots, queries.shape[1])
    far = swapped(own, "feat", 2)
    near = swapped(jnp.stack([own, far]), "feat", 1)
    parts = jnp.stack([own, far, near[0], near[1]])
    order = jnp.array([0, 2, 1, 3], jnp.int32)[jnp.arange(feats, dtype=jnp.int32) ^ feat_index]
    query_full = jnp.swapaxes(jnp.take(parts, order, axis=0), 0, 1).reshape(slots, feats * queries.shape[1])

    band_keys = jnp.stack([b[0] for b in blocks]).reshape(len(offsets) * rows, depth)
    band_labels = jnp.stack([b[1] for b in blocks]).reshape(len(offsets) * rows, feats * group)
    band_prior = band_labels[:, quarter]
    mask_row = band_mask[cluster_index]
    live_blocks = jnp.stack([mask_row[REACH + o] > 0 for o in offsets])
    live = jnp.repeat(live_blocks, rows)
    scale = temper / math.sqrt(depth)
    scores = jnp.einsum("qd,kd->qk", query_full, band_keys, preferred_element_type=jnp.float32) * scale
    scores = scores + band_prior.astype(jnp.float32)[None, :]
    scores = jnp.where(live[None, :], scores, -jnp.inf)
    top = jnp.max(scores, axis=1)
    weight = jnp.exp(scores - top[:, None])
    total = jnp.sum(weight, axis=1)
    accum = jnp.dot(weight.astype(jnp.bfloat16), band_labels, preferred_element_type=jnp.float32)

    column = lax.broadcasted_iota(jnp.int32, (slots, group), 1)

    def pack(part, top, total):
        for i, c in enumerate(split3(top) + split3(total)):
            part = jnp.where(column == quarter + i, c.astype(jnp.float32)[:, None], part)
        return part.astype(jnp.bfloat16)

    grid = accum.reshape(slots, feats, group)
    pick = lambda g: lax.dynamic_index_in_dim(grid, g, axis=1, keepdims=False)
    kept = jnp.stack([pick(feat_index), pick(feat_index ^ 2)])
    sent = jnp.stack([pack(pick(feat_index ^ 1), top, total), pack(pick(feat_index ^ 3), top, total)])
    message = swapped(sent, "feat", 1).astype(jnp.float32)
    other_top = join3([message[0, :, quarter + i] for i in range(3)])
    other_total = join3([message[0, :, quarter + 3 + i] for i in range(3)])
    highest = jnp.maximum(top, other_top)
    mine = jnp.exp(top - highest)
    theirs = jnp.exp(other_top - highest)
    kept = kept * mine[None, :, None] + message * theirs[None, :, None]
    top, total = highest, total * mine + other_total * theirs
    message = swapped(pack(kept[1], top, total), "feat", 2)
    kept, top, total = merge(kept[0], top, total, message, quarter)
    kept = kept[:, :quarter]
    shares = (kept / total[:, None]).astype(jnp.bfloat16)

    returned = lax.all_to_all(
        shares.reshape(clusters, capacity, quarter),
        "cluster",
        split_axis=0,
        concat_axis=0,
        tiled=True,
    )
    return jnp.dot(
        placed.T, returned.reshape(slots, quarter), preferred_element_type=jnp.float32
    ).astype(returned.dtype)


def solution(mesh):
    in_specs = (
        P("cluster", "feat"),
        P("cluster", None),
        P(),
        P(("cluster", "feat"), None),
        P(("cluster", "feat"), None),
        P(("cluster", "feat")),
    )
    out_specs = P("cluster", "feat")
    return jax.shard_map(body, mesh=mesh, in_specs=in_specs, out_specs=out_specs, check_vma=False)
```

```python
import math

import jax
import jax.numpy as jnp
from jax import lax
from jax.sharding import PartitionSpec as P

REACH = 3


temper = 2.0


def shifted(array, axis, by):
    peers = lax.axis_size(axis)
    return lax.ppermute(array, axis, [(i, (i - by) % peers) for i in range(peers)])


def swapped(array, axis, bit):
    peers = lax.axis_size(axis)
    return lax.ppermute(array, axis, [(i, i ^ bit) for i in range(peers)])


def round_bf16(x):
    return lax.reduce_precision(x, exponent_bits=8, mantissa_bits=7)


def split3(x):
    hi = round_bf16(x)
    rest = x - hi
    mid = round_bf16(rest)
    lo = rest - mid
    return [part.astype(jnp.bfloat16) for part in (hi, mid, lo)]


def join3(parts):
    hi, mid, lo = [p.astype(jnp.float32) for p in parts]
    return (hi + mid) + lo


def merge(kept, top, total, message, width):
    other = message.astype(jnp.float32)
    other_top = join3([other[:, width + i] for i in range(3)])
    other_total = join3([other[:, width + 3 + i] for i in range(3)])
    highest = jnp.maximum(top, other_top)
    mine = jnp.exp(top - highest)
    theirs = jnp.exp(other_top - highest)
    merged = kept * mine[:, None] + other * theirs[:, None]
    return merged, highest, total * mine + other_total * theirs


def body(queries, assign, band_mask, keys, labels, prior):
    clusters = lax.axis_size("cluster")
    cluster_index = lax.axis_index("cluster")
    feat_index = lax.axis_index("feat")
    feats = lax.axis_size("feat")
    local_rows = queries.shape[0]
    depth = keys.shape[1]
    classes = labels.shape[1]
    rows = keys.shape[0]
    capacity = 2 * local_rows // clusters
    slots = clusters * capacity

    quarter = classes // feats
    group = -(-(quarter + 6) // 128) * 128
    first = (lax.broadcasted_iota(jnp.int32, (rows, feats, group - quarter), 1) == 0) & (
        lax.broadcasted_iota(jnp.int32, (rows, feats, group - quarter), 2) == 0
    )
    spare = jnp.where(first, prior[:, None, None], jnp.zeros((), prior.dtype))
    grouped = jnp.concatenate([labels.reshape(rows, feats, quarter), spare], axis=2)
    block = jnp.stack([keys, grouped.reshape(rows, feats * group)])
    offsets = [0]
    for reach in range(1, REACH + 1):
        offsets += [reach, -reach]
    blocks = [block] + [shifted(block, "cluster", o) for o in offsets[1:]]

    target = assign[:, 0]
    onehot = (target[:, None] == jnp.arange(clusters, dtype=jnp.int32)[None, :]).astype(jnp.int32)
    before = jnp.cumsum(onehot, axis=0) - onehot
    position = target * capacity + jnp.sum(before * onehot, axis=1)
    placed = (lax.broadcasted_iota(jnp.int32, (slots, local_rows), 0) == position[None, :]).astype(queries.dtype)
    outgoing = jnp.dot(placed, queries, preferred_element_type=jnp.float32).astype(queries.dtype)
    arrived = lax.all_to_all(
        outgoing.reshape(clusters, capacity, queries.shape[1]),
        "cluster",
        split_axis=0,
        concat_axis=0,
        tiled=True,
    )
    band_keys = jnp.stack([b[0] for b in blocks]).reshape(len(offsets) * rows, depth)
    band_labels = jnp.stack([b[1] for b in blocks]).reshape(len(offsets) * rows, feats * group)
    arrived, band_keys, band_labels = lax.optimization_barrier((arrived, band_keys, band_labels))
    own = arrived.reshape(slots, queries.shape[1])
    far = swapped(own, "feat", 2)
    near = swapped(jnp.stack([own, far]), "feat", 1)
    parts = jnp.stack([own, far, near[0], near[1]])
    order = jnp.array([0, 2, 1, 3], jnp.int32)[jnp.arange(feats, dtype=jnp.int32) ^ feat_index]
    query_full = jnp.swapaxes(jnp.take(parts, order, axis=0), 0, 1).reshape(slots, feats * queries.shape[1])

    band_prior = band_labels[:, quarter]
    mask_row = band_mask[cluster_index]
    live_blocks = jnp.stack([mask_row[REACH + o] > 0 for o in offsets])
    live = jnp.repeat(live_blocks, rows)
    scale = temper / math.sqrt(depth)
    scores = jnp.einsum("qd,kd->qk", query_full, band_keys, preferred_element_type=jnp.float32) * scale
    scores = scores + band_prior.astype(jnp.float32)[None, :]
    scores = jnp.where(live[None, :], scores, -jnp.inf)
    top = jnp.max(scores, axis=1)
    weight = jnp.exp(scores - top[:, None])
    total = jnp.sum(weight, axis=1)
    accum = jnp.dot(weight.astype(jnp.bfloat16), band_labels, preferred_element_type=jnp.float32)

    column = lax.broadcasted_iota(jnp.int32, (slots, group), 1)

    def pack(part, top, total):
        for i, c in enumerate(split3(top) + split3(total)):
            part = jnp.where(column == quarter + i, c.astype(jnp.float32)[:, None], part)
        return part.astype(jnp.bfloat16)

    grid = accum.reshape(slots, feats, group)
    pick = lambda g: lax.dynamic_index_in_dim(grid, g, axis=1, keepdims=False)
    kept = jnp.stack([pick(feat_index), pick(feat_index ^ 2)])
    sent = jnp.stack([pack(pick(feat_index ^ 1), top, total), pack(pick(feat_index ^ 3), top, total)])
    message = swapped(sent, "feat", 1).astype(jnp.float32)
    other_top = join3([message[0, :, quarter + i] for i in range(3)])
    other_total = join3([message[0, :, quarter + 3 + i] for i in range(3)])
    highest = jnp.maximum(top, other_top)
    mine = jnp.exp(top - highest)
    theirs = jnp.exp(other_top - highest)
    kept = kept * mine[None, :, None] + message * theirs[None, :, None]
    top, total = highest, total * mine + other_total * theirs
    message = swapped(pack(kept[1], top, total), "feat", 2)
    kept, top, total = merge(kept[0], top, total, message, quarter)
    kept = kept[:, :quarter]
    shares = (kept / total[:, None]).astype(jnp.bfloat16)

    returned = lax.all_to_all(
        shares.reshape(clusters, capacity, quarter),
        "cluster",
        split_axis=0,
        concat_axis=0,
        tiled=True,
    )
    return jnp.dot(
        placed.T, returned.reshape(slots, quarter), preferred_element_type=jnp.float32
    ).astype(returned.dtype)


def solution(mesh):
    in_specs = (
        P("cluster", "feat"),
        P("cluster", None),
        P(),
        P(("cluster", "feat"), None),
        P(("cluster", "feat"), None),
        P(("cluster", "feat")),
    )
    out_specs = P("cluster", "feat")
    return jax.shard_map(body, mesh=mesh, in_specs=in_specs, out_specs=out_specs, check_vma=False)
```

```python
import math

import jax
import jax.numpy as jnp
from jax import lax
from jax.sharding import PartitionSpec as P

REACH = 3


temper = 2.0


def shifted(array, axis, by):
    peers = lax.axis_size(axis)
    return lax.ppermute(array, axis, [(i, (i - by) % peers) for i in range(peers)])


def swapped(array, axis, bit):
    peers = lax.axis_size(axis)
    return lax.ppermute(array, axis, [(i, i ^ bit) for i in range(peers)])


def round_bf16(x):
    return lax.reduce_precision(x, exponent_bits=8, mantissa_bits=7)


def split3(x):
    hi = round_bf16(x)
    rest = x - hi
    mid = round_bf16(rest)
    lo = rest - mid
    return [part.astype(jnp.bfloat16) for part in (hi, mid, lo)]


def join3(parts):
    hi, mid, lo = [p.astype(jnp.float32) for p in parts]
    return (hi + mid) + lo


def merge(kept, top, total, message, width):
    other = message.astype(jnp.float32)
    other_top = join3([other[:, width + i] for i in range(3)])
    other_total = join3([other[:, width + 3 + i] for i in range(3)])
    highest = jnp.maximum(top, other_top)
    mine = jnp.exp(top - highest)
    theirs = jnp.exp(other_top - highest)
    merged = kept * mine[:, None] + other * theirs[:, None]
    return merged, highest, total * mine + other_total * theirs


def body(queries, assign, band_mask, keys, labels, prior):
    clusters = lax.axis_size("cluster")
    cluster_index = lax.axis_index("cluster")
    feat_index = lax.axis_index("feat")
    feats = lax.axis_size("feat")
    local_rows = queries.shape[0]
    depth = keys.shape[1]
    classes = labels.shape[1]
    rows = keys.shape[0]
    capacity = 2 * local_rows // clusters
    slots = clusters * capacity

    quarter = classes // feats
    group = -(-(quarter + 6) // 128) * 128
    first = (lax.broadcasted_iota(jnp.int32, (rows, feats, group - quarter), 1) == 0) & (
        lax.broadcasted_iota(jnp.int32, (rows, feats, group - quarter), 2) == 0
    )
    spare = jnp.where(first, prior[:, None, None], jnp.zeros((), prior.dtype))
    grouped = jnp.concatenate([labels.reshape(rows, feats, quarter), spare], axis=2)
    block = jnp.stack([keys, grouped.reshape(rows, feats * group)])
    offsets = [0]
    for reach in range(1, REACH + 1):
        offsets += [reach, -reach]
    blocks = [block] + [shifted(block, "cluster", o) for o in offsets[1:]]

    target = assign[:, 0]
    onehot = (target[:, None] == jnp.arange(clusters, dtype=jnp.int32)[None, :]).astype(jnp.int32)
    before = jnp.cumsum(onehot, axis=0) - onehot
    position = target * capacity + jnp.sum(before * onehot, axis=1)
    placed = (lax.broadcasted_iota(jnp.int32, (slots, local_rows), 0) == position[None, :]).astype(queries.dtype)
    outgoing = jnp.dot(placed, queries, preferred_element_type=jnp.float32).astype(queries.dtype)
    arrived = lax.all_to_all(
        outgoing.reshape(clusters, capacity, queries.shape[1]),
        "cluster",
        split_axis=0,
        concat_axis=0,
        tiled=True,
    )
    own = arrived.reshape(slots, queries.shape[1])
    far = swapped(own, "feat", 2)
    near = swapped(jnp.stack([own, far]), "feat", 1)
    width = queries.shape[1]
    query_full = jnp.zeros((slots, feats * width), queries.dtype)
    for part, code in ((own, 0), (far, 2), (near[0], 1), (near[1], 3)):
        query_full = lax.dynamic_update_slice_in_dim(query_full, part, (feat_index ^ code) * width, axis=1)

    band_keys = jnp.stack([b[0] for b in blocks]).reshape(len(offsets) * rows, depth)
    band_labels = jnp.stack([b[1] for b in blocks]).reshape(len(offsets) * rows, feats * group)
    band_prior = band_labels[:, quarter]
    mask_row = band_mask[cluster_index]
    live_blocks = jnp.stack([mask_row[REACH + o] > 0 for o in offsets])
    live = jnp.repeat(live_blocks, rows)
    scale = temper / math.sqrt(depth)
    scores = jnp.einsum("qd,kd->qk", query_full, band_keys, preferred_element_type=jnp.float32) * scale
    scores = scores + band_prior.astype(jnp.float32)[None, :]
    scores = jnp.where(live[None, :], scores, -jnp.inf)
    top = jnp.max(scores, axis=1)
    weight = jnp.exp(scores - top[:, None])
    total = jnp.sum(weight, axis=1)
    accum = jnp.dot(weight.astype(jnp.bfloat16), band_labels, preferred_element_type=jnp.float32)

    column = lax.broadcasted_iota(jnp.int32, (slots, group), 1)

    def pack(part, top, total):
        for i, c in enumerate(split3(top) + split3(total)):
            part = jnp.where(column == quarter + i, c.astype(jnp.float32)[:, None], part)
        return part.astype(jnp.bfloat16)

    grid = accum.reshape(slots, feats, group)
    pick = lambda g: lax.dynamic_index_in_dim(grid, g, axis=1, keepdims=False)
    kept = jnp.stack([pick(feat_index), pick(feat_index ^ 2)])
    sent = jnp.stack([pack(pick(feat_index ^ 1), top, total), pack(pick(feat_index ^ 3), top, total)])
    message = swapped(sent, "feat", 1).astype(jnp.float32)
    other_top = join3([message[0, :, quarter + i] for i in range(3)])
    other_total = join3([message[0, :, quarter + 3 + i] for i in range(3)])
    highest = jnp.maximum(top, other_top)
    mine = jnp.exp(top - highest)
    theirs = jnp.exp(other_top - highest)
    kept = kept * mine[None, :, None] + message * theirs[None, :, None]
    top, total = highest, total * mine + other_total * theirs
    message = swapped(pack(kept[1], top, total), "feat", 2)
    kept, top, total = merge(kept[0], top, total, message, quarter)
    kept = kept[:, :quarter]
    shares = (kept / total[:, None]).astype(jnp.bfloat16)

    returned = lax.all_to_all(
        shares.reshape(clusters, capacity, quarter),
        "cluster",
        split_axis=0,
        concat_axis=0,
        tiled=True,
    )
    return jnp.dot(
        placed.T, returned.reshape(slots, quarter), preferred_element_type=jnp.float32
    ).astype(returned.dtype)


def solution(mesh):
    in_specs = (
        P("cluster", "feat"),
        P("cluster", None),
        P(),
        P(("cluster", "feat"), None),
        P(("cluster", "feat"), None),
        P(("cluster", "feat")),
    )
    out_specs = P("cluster", "feat")
    return jax.shard_map(body, mesh=mesh, in_specs=in_specs, out_specs=out_specs, check_vma=False)
```

```python
import math

import jax
import jax.numpy as jnp
from jax import lax
from jax.sharding import PartitionSpec as P

REACH = 3


temper = 2.0


def shifted(array, axis, by):
    peers = lax.axis_size(axis)
    return lax.ppermute(array, axis, [(i, (i - by) % peers) for i in range(peers)])


def swapped(array, axis, bit):
    peers = lax.axis_size(axis)
    return lax.ppermute(array, axis, [(i, i ^ bit) for i in range(peers)])


def round_bf16(x):
    return lax.reduce_precision(x, exponent_bits=8, mantissa_bits=7)


def split3(x):
    hi = round_bf16(x)
    rest = x - hi
    mid = round_bf16(rest)
    lo = rest - mid
    return [part.astype(jnp.bfloat16) for part in (hi, mid, lo)]


def join3(parts):
    hi, mid, lo = [p.astype(jnp.float32) for p in parts]
    return (hi + mid) + lo


def merge(kept, top, total, message, width):
    other = message.astype(jnp.float32)
    other_top = join3([other[:, width + i] for i in range(3)])
    other_total = join3([other[:, width + 3 + i] for i in range(3)])
    highest = jnp.maximum(top, other_top)
    mine = jnp.exp(top - highest)
    theirs = jnp.exp(other_top - highest)
    merged = kept * mine[:, None] + other * theirs[:, None]
    return merged, highest, total * mine + other_total * theirs


def body(queries, assign, band_mask, keys, labels, prior):
    clusters = lax.axis_size("cluster")
    cluster_index = lax.axis_index("cluster")
    feat_index = lax.axis_index("feat")
    feats = lax.axis_size("feat")
    local_rows = queries.shape[0]
    depth = keys.shape[1]
    classes = labels.shape[1]
    rows = keys.shape[0]
    capacity = 2 * local_rows // clusters
    slots = clusters * capacity

    quarter = classes // feats
    group = -(-(quarter + 6) // 128) * 128
    first = (lax.broadcasted_iota(jnp.int32, (rows, feats, group - quarter), 1) == 0) & (
        lax.broadcasted_iota(jnp.int32, (rows, feats, group - quarter), 2) == 0
    )
    spare = jnp.where(first, prior[:, None, None], jnp.zeros((), prior.dtype))
    grouped = jnp.concatenate([labels.reshape(rows, feats, quarter), spare], axis=2)
    block = jnp.stack([keys, grouped.reshape(rows, feats * group)])
    offsets = [0]
    for reach in sorted(range(1, REACH + 1), key=lambda r: r == 2):
        offsets += [reach, -reach]
    blocks = [block] + [shifted(block, "cluster", o) for o in offsets[1:]]

    target = assign[:, 0]
    onehot = (target[:, None] == jnp.arange(clusters, dtype=jnp.int32)[None, :]).astype(jnp.int32)
    before = jnp.cumsum(onehot, axis=0) - onehot
    position = target * capacity + jnp.sum(before * onehot, axis=1)
    placed = (lax.broadcasted_iota(jnp.int32, (slots, local_rows), 0) == position[None, :]).astype(queries.dtype)
    outgoing = jnp.dot(placed, queries, preferred_element_type=jnp.float32).astype(queries.dtype)
    arrived = lax.all_to_all(
        outgoing.reshape(clusters, capacity, queries.shape[1]),
        "cluster",
        split_axis=0,
        concat_axis=0,
        tiled=True,
    )
    own = arrived.reshape(slots, queries.shape[1])
    far = swapped(own, "feat", 2)
    near = swapped(jnp.stack([own, far]), "feat", 1)
    width = queries.shape[1]
    query_full = jnp.zeros((slots, feats * width), queries.dtype)
    for part, code in ((own, 0), (far, 2), (near[0], 1), (near[1], 3)):
        query_full = lax.dynamic_update_slice_in_dim(query_full, part, (feat_index ^ code) * width, axis=1)

    band_keys = jnp.stack([b[0] for b in blocks]).reshape(len(offsets) * rows, depth)
    band_labels = jnp.stack([b[1] for b in blocks]).reshape(len(offsets) * rows, feats * group)
    band_prior = band_labels[:, quarter]
    mask_row = band_mask[cluster_index]
    live_blocks = jnp.stack([mask_row[REACH + o] > 0 for o in offsets])
    live = jnp.repeat(live_blocks, rows)
    scale = temper / math.sqrt(depth)
    scores = jnp.einsum("qd,kd->qk", query_full, band_keys, preferred_element_type=jnp.float32) * scale
    scores = scores + band_prior.astype(jnp.float32)[None, :]
    scores = jnp.where(live[None, :], scores, -jnp.inf)
    top = jnp.max(scores, axis=1)
    weight = jnp.exp(scores - top[:, None])
    total = jnp.sum(weight, axis=1)
    accum = jnp.dot(weight.astype(jnp.bfloat16), band_labels, preferred_element_type=jnp.float32)

    column = lax.broadcasted_iota(jnp.int32, (slots, group), 1)

    def pack(part, top, total):
        for i, c in enumerate(split3(top) + split3(total)):
            part = jnp.where(column == quarter + i, c.astype(jnp.float32)[:, None], part)
        return part.astype(jnp.bfloat16)

    grid = accum.reshape(slots, feats, group)
    pick = lambda g: lax.dynamic_index_in_dim(grid, g, axis=1, keepdims=False)
    kept = jnp.stack([pick(feat_index), pick(feat_index ^ 2)])
    sent = jnp.stack([pack(pick(feat_index ^ 1), top, total), pack(pick(feat_index ^ 3), top, total)])
    message = swapped(sent, "feat", 1).astype(jnp.float32)
    other_top = join3([message[0, :, quarter + i] for i in range(3)])
    other_total = join3([message[0, :, quarter + 3 + i] for i in range(3)])
    highest = jnp.maximum(top, other_top)
    mine = jnp.exp(top - highest)
    theirs = jnp.exp(other_top - highest)
    kept = kept * mine[None, :, None] + message * theirs[None, :, None]
    top, total = highest, total * mine + other_total * theirs
    message = swapped(pack(kept[1], top, total), "feat", 2)
    kept, top, total = merge(kept[0], top, total, message, quarter)
    kept = kept[:, :quarter]
    shares = (kept / total[:, None]).astype(jnp.bfloat16)

    returned = lax.all_to_all(
        shares.reshape(clusters, capacity, quarter),
        "cluster",
        split_axis=0,
        concat_axis=0,
        tiled=True,
    )
    return jnp.dot(
        placed.T, returned.reshape(slots, quarter), preferred_element_type=jnp.float32
    ).astype(returned.dtype)


def solution(mesh):
    in_specs = (
        P("cluster", "feat"),
        P("cluster", None),
        P(),
        P(("cluster", "feat"), None),
        P(("cluster", "feat"), None),
        P(("cluster", "feat")),
    )
    out_specs = P("cluster", "feat")
    return jax.shard_map(body, mesh=mesh, in_specs=in_specs, out_specs=out_specs, check_vma=False)
```

```python
import math

import jax
import jax.numpy as jnp
from jax import lax
from jax.sharding import PartitionSpec as P

REACH = 3


temper = 2.0


def shifted(array, axis, by):
    peers = lax.axis_size(axis)
    return lax.ppermute(array, axis, [(i, (i - by) % peers) for i in range(peers)])


def swapped(array, axis, bit):
    peers = lax.axis_size(axis)
    return lax.ppermute(array, axis, [(i, i ^ bit) for i in range(peers)])


def round_bf16(x):
    return lax.reduce_precision(x, exponent_bits=8, mantissa_bits=7)


def split3(x):
    hi = round_bf16(x)
    rest = x - hi
    mid = round_bf16(rest)
    lo = rest - mid
    return [part.astype(jnp.bfloat16) for part in (hi, mid, lo)]


def join3(parts):
    hi, mid, lo = [p.astype(jnp.float32) for p in parts]
    return (hi + mid) + lo


def merge(kept, top, total, message, width):
    other = message.astype(jnp.float32)
    other_top = join3([other[:, width + i] for i in range(3)])
    other_total = join3([other[:, width + 3 + i] for i in range(3)])
    highest = jnp.maximum(top, other_top)
    mine = jnp.exp(top - highest)
    theirs = jnp.exp(other_top - highest)
    merged = kept * mine[:, None] + other * theirs[:, None]
    return merged, highest, total * mine + other_total * theirs


def body(queries, assign, band_mask, keys, labels, prior):
    clusters = lax.axis_size("cluster")
    cluster_index = lax.axis_index("cluster")
    feat_index = lax.axis_index("feat")
    feats = lax.axis_size("feat")
    local_rows = queries.shape[0]
    depth = keys.shape[1]
    classes = labels.shape[1]
    rows = keys.shape[0]
    capacity = 2 * local_rows // clusters
    slots = clusters * capacity

    quarter = classes // feats
    group = -(-(quarter + 6) // 128) * 128
    first = (lax.broadcasted_iota(jnp.int32, (rows, feats, group - quarter), 1) == 0) & (
        lax.broadcasted_iota(jnp.int32, (rows, feats, group - quarter), 2) == 0
    )
    spare = jnp.where(first, prior[:, None, None], jnp.zeros((), prior.dtype))
    grouped = jnp.concatenate([labels.reshape(rows, feats, quarter), spare], axis=2)
    block = jnp.stack([keys, grouped.reshape(rows, feats * group)])
    offsets = [0]
    for reach in sorted(range(1, REACH + 1), key=lambda r: r == 2):
        offsets += [reach, -reach]
    blocks = [block] + [shifted(block, "cluster", o) for o in offsets[1:]]

    target = assign[:, 0]
    onehot = (target[:, None] == jnp.arange(clusters, dtype=jnp.int32)[None, :]).astype(jnp.int32)
    before = jnp.cumsum(onehot, axis=0) - onehot
    position = target * capacity + jnp.sum(before * onehot, axis=1)
    placed = (lax.broadcasted_iota(jnp.int32, (slots, local_rows), 0) == position[None, :]).astype(queries.dtype)
    outgoing = jnp.dot(placed, queries, preferred_element_type=jnp.float32).astype(queries.dtype)
    arrived = lax.all_to_all(
        outgoing.reshape(clusters, capacity, queries.shape[1]),
        "cluster",
        split_axis=0,
        concat_axis=0,
        tiled=True,
    )
    own = arrived.reshape(slots, queries.shape[1])
    far = swapped(own, "feat", 2)
    near = swapped(jnp.stack([own, far]), "feat", 1)
    width = queries.shape[1]
    query_full = jnp.zeros((slots, feats * width), queries.dtype)
    for part, code in ((own, 0), (far, 2), (near[0], 1), (near[1], 3)):
        query_full = lax.dynamic_update_slice_in_dim(query_full, part, (feat_index ^ code) * width, axis=1)

    band_keys = jnp.stack([b[0] for b in blocks]).reshape(len(offsets) * rows, depth)
    band_labels = jnp.concatenate([b[1].T for b in blocks], axis=1)
    band_prior = jnp.concatenate([b[1][:, quarter] for b in blocks])
    mask_row = band_mask[cluster_index]
    live_blocks = jnp.stack([mask_row[REACH + o] > 0 for o in offsets])
    live = jnp.repeat(live_blocks, rows)
    scale = temper / math.sqrt(depth)
    scores = jnp.einsum("qd,kd->qk", query_full, band_keys, preferred_element_type=jnp.float32) * scale
    scores = scores + band_prior.astype(jnp.float32)[None, :]
    scores = jnp.where(live[None, :], scores, -jnp.inf)
    top = jnp.max(scores, axis=1)
    weight = jnp.exp(scores - top[:, None])
    total = jnp.sum(weight, axis=1)
    accum = jnp.einsum("qk,ck->qc", weight.astype(jnp.bfloat16), band_labels, preferred_element_type=jnp.float32)

    column = lax.broadcasted_iota(jnp.int32, (slots, group), 1)

    def pack(part, top, total):
        for i, c in enumerate(split3(top) + split3(total)):
            part = jnp.where(column == quarter + i, c.astype(jnp.float32)[:, None], part)
        return part.astype(jnp.bfloat16)

    grid = accum.reshape(slots, feats, group)
    pick = lambda g: lax.dynamic_index_in_dim(grid, g, axis=1, keepdims=False)
    kept = jnp.stack([pick(feat_index), pick(feat_index ^ 2)])
    sent = jnp.stack([pack(pick(feat_index ^ 1), top, total), pack(pick(feat_index ^ 3), top, total)])
    message = swapped(sent, "feat", 1).astype(jnp.float32)
    other_top = join3([message[0, :, quarter + i] for i in range(3)])
    other_total = join3([message[0, :, quarter + 3 + i] for i in range(3)])
    highest = jnp.maximum(top, other_top)
    mine = jnp.exp(top - highest)
    theirs = jnp.exp(other_top - highest)
    kept = kept * mine[None, :, None] + message * theirs[None, :, None]
    top, total = highest, total * mine + other_total * theirs
    message = swapped(pack(kept[1], top, total), "feat", 2)
    kept, top, total = merge(kept[0], top, total, message, quarter)
    kept = kept[:, :quarter]
    shares = (kept / total[:, None]).astype(jnp.bfloat16)

    returned = lax.all_to_all(
        shares.reshape(clusters, capacity, quarter),
        "cluster",
        split_axis=0,
        concat_axis=0,
        tiled=True,
    )
    return jnp.dot(
        placed.T, returned.reshape(slots, quarter), preferred_element_type=jnp.float32
    ).astype(returned.dtype)


def solution(mesh):
    in_specs = (
        P("cluster", "feat"),
        P("cluster", None),
        P(),
        P(("cluster", "feat"), None),
        P(("cluster", "feat"), None),
        P(("cluster", "feat")),
    )
    out_specs = P("cluster", "feat")
    return jax.shard_map(body, mesh=mesh, in_specs=in_specs, out_specs=out_specs, check_vma=False)
```

```python
import math

import jax
import jax.numpy as jnp
from jax import lax
from jax.sharding import PartitionSpec as P

REACH = 3


temper = 2.0


def shifted(array, axis, by):
    peers = lax.axis_size(axis)
    return lax.ppermute(array, axis, [(i, (i - by) % peers) for i in range(peers)])


def swapped(array, axis, bit):
    peers = lax.axis_size(axis)
    return lax.ppermute(array, axis, [(i, i ^ bit) for i in range(peers)])


def round_bf16(x):
    return lax.reduce_precision(x, exponent_bits=8, mantissa_bits=7)


def split3(x):
    hi = round_bf16(x)
    rest = x - hi
    mid = round_bf16(rest)
    lo = rest - mid
    return [part.astype(jnp.bfloat16) for part in (hi, mid, lo)]


def join3(parts):
    hi, mid, lo = [p.astype(jnp.float32) for p in parts]
    return (hi + mid) + lo


def merge(kept, top, total, message, width):
    other = message.astype(jnp.float32)
    other_top = join3([other[:, width + i] for i in range(3)])
    other_total = join3([other[:, width + 3 + i] for i in range(3)])
    highest = jnp.maximum(top, other_top)
    mine = jnp.exp(top - highest)
    theirs = jnp.exp(other_top - highest)
    merged = kept * mine[:, None] + other * theirs[:, None]
    return merged, highest, total * mine + other_total * theirs


def body(queries, assign, band_mask, keys, labels, prior):
    clusters = lax.axis_size("cluster")
    cluster_index = lax.axis_index("cluster")
    feat_index = lax.axis_index("feat")
    feats = lax.axis_size("feat")
    local_rows = queries.shape[0]
    depth = keys.shape[1]
    classes = labels.shape[1]
    rows = keys.shape[0]
    capacity = 2 * local_rows // clusters
    slots = clusters * capacity

    quarter = classes // feats
    group = -(-(quarter + 6) // 128) * 128
    first = (lax.broadcasted_iota(jnp.int32, (rows, feats, group - quarter), 1) == 0) & (
        lax.broadcasted_iota(jnp.int32, (rows, feats, group - quarter), 2) == 0
    )
    spare = jnp.where(first, prior[:, None, None], jnp.zeros((), prior.dtype))
    grouped = jnp.concatenate([labels.reshape(rows, feats, quarter), spare], axis=2)
    block = jnp.stack([keys, grouped.reshape(rows, feats * group)])
    offsets = [0]
    for reach in sorted(range(1, REACH + 1), key=lambda r: (r == 2, -r)):
        offsets += [reach, -reach]
    blocks = [block] + [shifted(block, "cluster", o) for o in offsets[1:]]

    target = assign[:, 0]
    onehot = (target[:, None] == jnp.arange(clusters, dtype=jnp.int32)[None, :]).astype(jnp.int32)
    before = jnp.cumsum(onehot, axis=0) - onehot
    position = target * capacity + jnp.sum(before * onehot, axis=1)
    placed = (lax.broadcasted_iota(jnp.int32, (slots, local_rows), 0) == position[None, :]).astype(queries.dtype)
    outgoing = jnp.dot(placed, queries, preferred_element_type=jnp.float32).astype(queries.dtype)
    arrived = lax.all_to_all(
        outgoing.reshape(clusters, capacity, queries.shape[1]),
        "cluster",
        split_axis=0,
        concat_axis=0,
        tiled=True,
    )
    own = arrived.reshape(slots, queries.shape[1])
    far = swapped(own, "feat", 2)
    near = swapped(jnp.stack([own, far]), "feat", 1)
    width = queries.shape[1]
    query_full = jnp.zeros((slots, feats * width), queries.dtype)
    for part, code in ((own, 0), (far, 2), (near[0], 1), (near[1], 3)):
        query_full = lax.dynamic_update_slice_in_dim(query_full, part, (feat_index ^ code) * width, axis=1)

    band_keys = jnp.stack([b[0] for b in blocks]).reshape(len(offsets) * rows, depth)
    band_labels = jnp.stack([b[1] for b in blocks]).reshape(len(offsets) * rows, feats * group)
    band_prior = band_labels[:, quarter]
    mask_row = band_mask[cluster_index]
    live_blocks = jnp.stack([mask_row[REACH + o] > 0 for o in offsets])
    live = jnp.repeat(live_blocks, rows)
    scale = temper / math.sqrt(depth)
    scores = jnp.einsum("qd,kd->qk", query_full, band_keys, preferred_element_type=jnp.float32) * scale
    scores = scores + band_prior.astype(jnp.float32)[None, :]
    scores = jnp.where(live[None, :], scores, -jnp.inf)
    top = jnp.max(scores, axis=1)
    weight = jnp.exp(scores - top[:, None])
    total = jnp.sum(weight, axis=1)
    accum = jnp.dot(weight.astype(jnp.bfloat16), band_labels, preferred_element_type=jnp.float32)

    column = lax.broadcasted_iota(jnp.int32, (slots, group), 1)

    def pack(part, top, total):
        for i, c in enumerate(split3(top) + split3(total)):
            part = jnp.where(column == quarter + i, c.astype(jnp.float32)[:, None], part)
        return part.astype(jnp.bfloat16)

    grid = accum.reshape(slots, feats, group)
    pick = lambda g: lax.dynamic_index_in_dim(grid, g, axis=1, keepdims=False)
    kept = jnp.stack([pick(feat_index), pick(feat_index ^ 2)])
    sent = jnp.stack([pack(pick(feat_index ^ 1), top, total), pack(pick(feat_index ^ 3), top, total)])
    message = swapped(sent, "feat", 1).astype(jnp.float32)
    other_top = join3([message[0, :, quarter + i] for i in range(3)])
    other_total = join3([message[0, :, quarter + 3 + i] for i in range(3)])
    highest = jnp.maximum(top, other_top)
    mine = jnp.exp(top - highest)
    theirs = jnp.exp(other_top - highest)
    kept = kept * mine[None, :, None] + message * theirs[None, :, None]
    top, total = highest, total * mine + other_total * theirs
    message = swapped(pack(kept[1], top, total), "feat", 2)
    kept, top, total = merge(kept[0], top, total, message, quarter)
    kept = kept[:, :quarter]
    shares = (kept / total[:, None]).astype(jnp.bfloat16)

    returned = lax.all_to_all(
        shares.reshape(clusters, capacity, quarter),
        "cluster",
        split_axis=0,
        concat_axis=0,
        tiled=True,
    )
    return jnp.dot(
        placed.T, returned.reshape(slots, quarter), preferred_element_type=jnp.float32
    ).astype(returned.dtype)


def solution(mesh):
    in_specs = (
        P("cluster", "feat"),
        P("cluster", None),
        P(),
        P(("cluster", "feat"), None),
        P(("cluster", "feat"), None),
        P(("cluster", "feat")),
    )
    out_specs = P("cluster", "feat")
    return jax.shard_map(body, mesh=mesh, in_specs=in_specs, out_specs=out_specs, check_vma=False)
```

```python
import math

import jax
import jax.numpy as jnp
from jax import lax
from jax.sharding import PartitionSpec as P

REACH = 3


temper = 2.0


def shifted(array, axis, by):
    peers = lax.axis_size(axis)
    return lax.ppermute(array, axis, [(i, (i - by) % peers) for i in range(peers)])


def swapped(array, axis, bit):
    peers = lax.axis_size(axis)
    return lax.ppermute(array, axis, [(i, i ^ bit) for i in range(peers)])


def round_bf16(x):
    return lax.reduce_precision(x, exponent_bits=8, mantissa_bits=7)


def split3(x):
    hi = round_bf16(x)
    rest = x - hi
    mid = round_bf16(rest)
    lo = rest - mid
    return [part.astype(jnp.bfloat16) for part in (hi, mid, lo)]


def join3(parts):
    hi, mid, lo = [p.astype(jnp.float32) for p in parts]
    return (hi + mid) + lo


def merge(kept, top, total, message, width):
    other = message.astype(jnp.float32)
    other_top = join3([other[:, width + i] for i in range(3)])
    other_total = join3([other[:, width + 3 + i] for i in range(3)])
    highest = jnp.maximum(top, other_top)
    mine = jnp.exp(top - highest)
    theirs = jnp.exp(other_top - highest)
    merged = kept * mine[:, None] + other * theirs[:, None]
    return merged, highest, total * mine + other_total * theirs


def body(queries, assign, band_mask, keys, labels, prior):
    clusters = lax.axis_size("cluster")
    cluster_index = lax.axis_index("cluster")
    feat_index = lax.axis_index("feat")
    feats = lax.axis_size("feat")
    local_rows = queries.shape[0]
    depth = keys.shape[1]
    classes = labels.shape[1]
    rows = keys.shape[0]
    capacity = 2 * local_rows // clusters
    slots = clusters * capacity

    quarter = classes // feats
    group = -(-(quarter + 6) // 128) * 128
    lane = lax.broadcasted_iota(jnp.int32, (rows, feats * group), 1)
    padded = jnp.pad(labels.reshape(rows, feats, quarter), ((0, 0), (0, 0), (0, group - quarter)))
    grouped = jnp.where(lane == quarter, prior[:, None], padded.reshape(rows, feats * group))
    block = jnp.stack([keys, grouped])
    offsets = [0]
    for reach in sorted(range(1, REACH + 1), key=lambda r: (r == 2, -r)):
        offsets += [reach, -reach]
    blocks = [block] + [shifted(block, "cluster", o) for o in offsets[1:]]

    target = assign[:, 0]
    onehot = (target[:, None] == jnp.arange(clusters, dtype=jnp.int32)[None, :]).astype(jnp.int32)
    before = jnp.cumsum(onehot, axis=0) - onehot
    position = target * capacity + jnp.sum(before * onehot, axis=1)
    placed = (lax.broadcasted_iota(jnp.int32, (slots, local_rows), 0) == position[None, :]).astype(queries.dtype)
    outgoing = jnp.dot(placed, queries, preferred_element_type=jnp.float32).astype(queries.dtype)
    arrived = lax.all_to_all(
        outgoing.reshape(clusters, capacity, queries.shape[1]),
        "cluster",
        split_axis=0,
        concat_axis=0,
        tiled=True,
    )
    own = arrived.reshape(slots, queries.shape[1])
    far = swapped(own, "feat", 2)
    near = swapped(jnp.stack([own, far]), "feat", 1)
    width = queries.shape[1]
    query_full = jnp.zeros((slots, feats * width), queries.dtype)
    for part, code in ((own, 0), (far, 2), (near[0], 1), (near[1], 3)):
        query_full = lax.dynamic_update_slice_in_dim(query_full, part, (feat_index ^ code) * width, axis=1)

    band_keys = jnp.stack([b[0] for b in blocks]).reshape(len(offsets) * rows, depth)
    band_labels = jnp.stack([b[1] for b in blocks]).reshape(len(offsets) * rows, feats * group)
    band_prior = band_labels[:, quarter]
    mask_row = band_mask[cluster_index]
    live_blocks = jnp.stack([mask_row[REACH + o] > 0 for o in offsets])
    live = jnp.repeat(live_blocks, rows)
    scale = temper / math.sqrt(depth)
    scores = jnp.einsum("qd,kd->qk", query_full, band_keys, preferred_element_type=jnp.float32) * scale
    scores = scores + band_prior.astype(jnp.float32)[None, :]
    scores = jnp.where(live[None, :], scores, -jnp.inf)
    top = jnp.max(scores, axis=1)
    weight = jnp.exp(scores - top[:, None])
    total = jnp.sum(weight, axis=1)
    accum = jnp.dot(weight.astype(jnp.bfloat16), band_labels, preferred_element_type=jnp.float32)

    column = lax.broadcasted_iota(jnp.int32, (slots, group), 1)

    def pack(part, top, total):
        for i, c in enumerate(split3(top) + split3(total)):
            part = jnp.where(column == quarter + i, c.astype(jnp.float32)[:, None], part)
        return part.astype(jnp.bfloat16)

    grid = accum.reshape(slots, feats, group)
    pick = lambda g: lax.dynamic_index_in_dim(grid, g, axis=1, keepdims=False)
    kept = jnp.stack([pick(feat_index), pick(feat_index ^ 2)])
    sent = jnp.stack([pack(pick(feat_index ^ 1), top, total), pack(pick(feat_index ^ 3), top, total)])
    message = swapped(sent, "feat", 1).astype(jnp.float32)
    other_top = join3([message[0, :, quarter + i] for i in range(3)])
    other_total = join3([message[0, :, quarter + 3 + i] for i in range(3)])
    highest = jnp.maximum(top, other_top)
    mine = jnp.exp(top - highest)
    theirs = jnp.exp(other_top - highest)
    kept = kept * mine[None, :, None] + message * theirs[None, :, None]
    top, total = highest, total * mine + other_total * theirs
    message = swapped(pack(kept[1], top, total), "feat", 2)
    kept, top, total = merge(kept[0], top, total, message, quarter)
    kept = kept[:, :quarter]
    shares = (kept / total[:, None]).astype(jnp.bfloat16)

    returned = lax.all_to_all(
        shares.reshape(clusters, capacity, quarter),
        "cluster",
        split_axis=0,
        concat_axis=0,
        tiled=True,
    )
    return jnp.dot(
        placed.T, returned.reshape(slots, quarter), preferred_element_type=jnp.float32
    ).astype(returned.dtype)


def solution(mesh):
    in_specs = (
        P("cluster", "feat"),
        P("cluster", None),
        P(),
        P(("cluster", "feat"), None),
        P(("cluster", "feat"), None),
        P(("cluster", "feat")),
    )
    out_specs = P("cluster", "feat")
    return jax.shard_map(body, mesh=mesh, in_specs=in_specs, out_specs=out_specs, check_vma=False)
```

```python
import math

import jax
import jax.numpy as jnp
from jax import lax
from jax.sharding import PartitionSpec as P

REACH = 3


temper = 2.0


def shifted(array, axis, by):
    peers = lax.axis_size(axis)
    return lax.ppermute(array, axis, [(i, (i - by) % peers) for i in range(peers)])


def swapped(array, axis, bit):
    peers = lax.axis_size(axis)
    return lax.ppermute(array, axis, [(i, i ^ bit) for i in range(peers)])


def round_bf16(x):
    return lax.reduce_precision(x, exponent_bits=8, mantissa_bits=7)


def split3(x):
    hi = round_bf16(x)
    rest = x - hi
    mid = round_bf16(rest)
    lo = rest - mid
    return [part.astype(jnp.bfloat16) for part in (hi, mid, lo)]


def join3(parts):
    hi, mid, lo = [p.astype(jnp.float32) for p in parts]
    return (hi + mid) + lo


def merge(kept, top, total, message, width):
    other = message.astype(jnp.float32)
    other_top = join3([other[:, width + i] for i in range(3)])
    other_total = join3([other[:, width + 3 + i] for i in range(3)])
    highest = jnp.maximum(top, other_top)
    mine = jnp.exp(top - highest)
    theirs = jnp.exp(other_top - highest)
    merged = kept * mine[:, None] + other * theirs[:, None]
    return merged, highest, total * mine + other_total * theirs


def body(queries, assign, band_mask, keys, labels, prior):
    clusters = lax.axis_size("cluster")
    cluster_index = lax.axis_index("cluster")
    feat_index = lax.axis_index("feat")
    feats = lax.axis_size("feat")
    local_rows = queries.shape[0]
    depth = keys.shape[1]
    classes = labels.shape[1]
    rows = keys.shape[0]
    capacity = 2 * local_rows // clusters
    slots = clusters * capacity

    quarter = classes // feats
    group = -(-(quarter + 6) // 128) * 128
    lane = lax.broadcasted_iota(jnp.int32, (2, rows, feats * group), 2)
    plane = lax.broadcasted_iota(jnp.int32, (2, rows, feats * group), 0)
    padded = jnp.pad(labels.reshape(rows, feats, quarter), ((0, 0), (0, 0), (0, group - quarter)))
    grouped = jnp.where(lane == quarter, prior[None, :, None], padded.reshape(1, rows, feats * group))
    block = jnp.where(plane == 0, keys[None], grouped)
    offsets = [0]
    for reach in sorted(range(1, REACH + 1), key=lambda r: (r == 2, -r)):
        offsets += [reach, -reach]
    blocks = [block] + [shifted(block, "cluster", o) for o in offsets[1:]]

    target = assign[:, 0]
    onehot = (target[:, None] == jnp.arange(clusters, dtype=jnp.int32)[None, :]).astype(jnp.int32)
    before = jnp.cumsum(onehot, axis=0) - onehot
    position = target * capacity + jnp.sum(before * onehot, axis=1)
    placed = (lax.broadcasted_iota(jnp.int32, (slots, local_rows), 0) == position[None, :]).astype(queries.dtype)
    outgoing = jnp.dot(placed, queries, preferred_element_type=jnp.float32).astype(queries.dtype)
    arrived = lax.all_to_all(
        outgoing.reshape(clusters, capacity, queries.shape[1]),
        "cluster",
        split_axis=0,
        concat_axis=0,
        tiled=True,
    )
    own = arrived.reshape(slots, queries.shape[1])
    far = swapped(own, "feat", 2)
    near = swapped(jnp.stack([own, far]), "feat", 1)
    width = queries.shape[1]
    query_full = jnp.zeros((slots, feats * width), queries.dtype)
    for part, code in ((own, 0), (far, 2), (near[0], 1), (near[1], 3)):
        query_full = lax.dynamic_update_slice_in_dim(query_full, part, (feat_index ^ code) * width, axis=1)

    band_keys = jnp.stack([b[0] for b in blocks]).reshape(len(offsets) * rows, depth)
    band_labels = jnp.stack([b[1] for b in blocks]).reshape(len(offsets) * rows, feats * group)
    band_prior = band_labels[:, quarter]
    mask_row = band_mask[cluster_index]
    live_blocks = jnp.stack([mask_row[REACH + o] > 0 for o in offsets])
    live = jnp.repeat(live_blocks, rows)
    scale = temper / math.sqrt(depth)
    scores = jnp.einsum("qd,kd->qk", query_full, band_keys, preferred_element_type=jnp.float32) * scale
    scores = scores + band_prior.astype(jnp.float32)[None, :]
    scores = jnp.where(live[None, :], scores, -jnp.inf)
    top = jnp.max(scores, axis=1)
    weight = jnp.exp(scores - top[:, None])
    total = jnp.sum(weight, axis=1)
    accum = jnp.dot(weight.astype(jnp.bfloat16), band_labels, preferred_element_type=jnp.float32)

    column = lax.broadcasted_iota(jnp.int32, (slots, group), 1)

    def pack(part, top, total):
        for i, c in enumerate(split3(top) + split3(total)):
            part = jnp.where(column == quarter + i, c.astype(jnp.float32)[:, None], part)
        return part.astype(jnp.bfloat16)

    grid = accum.reshape(slots, feats, group)
    pick = lambda g: lax.dynamic_index_in_dim(grid, g, axis=1, keepdims=False)
    kept = jnp.stack([pick(feat_index), pick(feat_index ^ 2)])
    sent = jnp.stack([pack(pick(feat_index ^ 1), top, total), pack(pick(feat_index ^ 3), top, total)])
    message = swapped(sent, "feat", 1).astype(jnp.float32)
    other_top = join3([message[0, :, quarter + i] for i in range(3)])
    other_total = join3([message[0, :, quarter + 3 + i] for i in range(3)])
    highest = jnp.maximum(top, other_top)
    mine = jnp.exp(top - highest)
    theirs = jnp.exp(other_top - highest)
    kept = kept * mine[None, :, None] + message * theirs[None, :, None]
    top, total = highest, total * mine + other_total * theirs
    message = swapped(pack(kept[1], top, total), "feat", 2)
    kept, top, total = merge(kept[0], top, total, message, quarter)
    kept = kept[:, :quarter]
    shares = (kept / total[:, None]).astype(jnp.bfloat16)

    returned = lax.all_to_all(
        shares.reshape(clusters, capacity, quarter),
        "cluster",
        split_axis=0,
        concat_axis=0,
        tiled=True,
    )
    return jnp.dot(
        placed.T, returned.reshape(slots, quarter), preferred_element_type=jnp.float32
    ).astype(returned.dtype)


def solution(mesh):
    in_specs = (
        P("cluster", "feat"),
        P("cluster", None),
        P(),
        P(("cluster", "feat"), None),
        P(("cluster", "feat"), None),
        P(("cluster", "feat")),
    )
    out_specs = P("cluster", "feat")
    return jax.shard_map(body, mesh=mesh, in_specs=in_specs, out_specs=out_specs, check_vma=False)
```

```python
import math

import jax
import jax.numpy as jnp
from jax import lax
from jax.sharding import PartitionSpec as P

REACH = 3


temper = 2.0


def shifted(array, axis, by):
    peers = lax.axis_size(axis)
    return lax.ppermute(array, axis, [(i, (i - by) % peers) for i in range(peers)])


def swapped(array, axis, bit):
    peers = lax.axis_size(axis)
    return lax.ppermute(array, axis, [(i, i ^ bit) for i in range(peers)])


def round_bf16(x):
    return lax.reduce_precision(x, exponent_bits=8, mantissa_bits=7)


def split3(x):
    hi = round_bf16(x)
    rest = x - hi
    mid = round_bf16(rest)
    lo = rest - mid
    return [part.astype(jnp.bfloat16) for part in (hi, mid, lo)]


def join3(parts):
    hi, mid, lo = [p.astype(jnp.float32) for p in parts]
    return (hi + mid) + lo


def merge(kept, top, total, message, width):
    other = message.astype(jnp.float32)
    other_top = join3([other[:, width + i] for i in range(3)])
    other_total = join3([other[:, width + 3 + i] for i in range(3)])
    highest = jnp.maximum(top, other_top)
    mine = jnp.exp(top - highest)
    theirs = jnp.exp(other_top - highest)
    merged = kept * mine[:, None] + other * theirs[:, None]
    return merged, highest, total * mine + other_total * theirs


def body(queries, assign, band_mask, keys, labels, prior):
    clusters = lax.axis_size("cluster")
    cluster_index = lax.axis_index("cluster")
    feat_index = lax.axis_index("feat")
    feats = lax.axis_size("feat")
    local_rows = queries.shape[0]
    depth = keys.shape[1]
    classes = labels.shape[1]
    rows = keys.shape[0]
    capacity = 2 * local_rows // clusters
    slots = clusters * capacity

    quarter = classes // feats
    group = -(-(quarter + 6) // 128) * 128
    lane = lax.broadcasted_iota(jnp.int32, (rows, feats * group), 1)
    padded = jnp.pad(labels.reshape(rows, feats, quarter), ((0, 0), (0, 0), (0, group - quarter)))
    grouped = jnp.where(lane == quarter, prior[:, None], padded.reshape(rows, feats * group))
    block = jnp.stack([keys, grouped])
    offsets = [0]
    for reach in sorted(range(1, REACH + 1), key=lambda r: (r == 2, -r)):
        offsets += [reach, -reach]
    blocks = [block] + [shifted(block, "cluster", o) for o in offsets[1:]]

    target = assign[:, 0]
    onehot = (target[:, None] == jnp.arange(clusters, dtype=jnp.int32)[None, :]).astype(jnp.int32)
    before = jnp.cumsum(onehot, axis=0) - onehot
    position = target * capacity + jnp.sum(before * onehot, axis=1)
    placed = (lax.broadcasted_iota(jnp.int32, (slots, local_rows), 0) == position[None, :]).astype(queries.dtype)
    outgoing = jnp.dot(placed, queries, preferred_element_type=jnp.float32).astype(queries.dtype)
    arrived = lax.all_to_all(
        outgoing.reshape(clusters, capacity, queries.shape[1]),
        "cluster",
        split_axis=0,
        concat_axis=0,
        tiled=True,
    )
    own = arrived.reshape(slots, queries.shape[1])
    far = swapped(own, "feat", 2)
    near = swapped(jnp.stack([own, far]), "feat", 1)
    width = queries.shape[1]
    query_full = jnp.zeros((slots, feats * width), queries.dtype)
    for part, code in ((own, 0), (far, 2), (near[0], 1), (near[1], 3)):
        query_full = lax.dynamic_update_slice_in_dim(query_full, part, (feat_index ^ code) * width, axis=1)

    band_keys = jnp.stack([b[0] for b in blocks]).reshape(len(offsets) * rows, depth)
    band_labels = jnp.stack([b[1] for b in blocks]).reshape(len(offsets) * rows, feats * group)
    band_prior = jnp.concatenate([b[1][:, quarter] for b in blocks])
    mask_row = band_mask[cluster_index]
    live_blocks = jnp.stack([mask_row[REACH + o] > 0 for o in offsets])
    live = jnp.repeat(live_blocks, rows)
    scale = temper / math.sqrt(depth)
    scores = jnp.einsum("qd,kd->qk", query_full, band_keys, preferred_element_type=jnp.float32) * scale
    scores = scores + band_prior.astype(jnp.float32)[None, :]
    scores = jnp.where(live[None, :], scores, -jnp.inf)
    top = jnp.max(scores, axis=1)
    weight = jnp.exp(scores - top[:, None])
    total = jnp.sum(weight, axis=1)
    accum = jnp.dot(weight.astype(jnp.bfloat16), band_labels, preferred_element_type=jnp.float32)

    column = lax.broadcasted_iota(jnp.int32, (slots, group), 1)

    def pack(part, top, total):
        for i, c in enumerate(split3(top) + split3(total)):
            part = jnp.where(column == quarter + i, c.astype(jnp.float32)[:, None], part)
        return part.astype(jnp.bfloat16)

    grid = accum.reshape(slots, feats, group)
    pick = lambda g: lax.dynamic_index_in_dim(grid, g, axis=1, keepdims=False)
    kept = jnp.stack([pick(feat_index), pick(feat_index ^ 2)])
    sent = jnp.stack([pack(pick(feat_index ^ 1), top, total), pack(pick(feat_index ^ 3), top, total)])
    message = swapped(sent, "feat", 1).astype(jnp.float32)
    other_top = join3([message[0, :, quarter + i] for i in range(3)])
    other_total = join3([message[0, :, quarter + 3 + i] for i in range(3)])
    highest = jnp.maximum(top, other_top)
    mine = jnp.exp(top - highest)
    theirs = jnp.exp(other_top - highest)
    kept = kept * mine[None, :, None] + message * theirs[None, :, None]
    top, total = highest, total * mine + other_total * theirs
    message = swapped(pack(kept[1], top, total), "feat", 2)
    kept, top, total = merge(kept[0], top, total, message, quarter)
    kept = kept[:, :quarter]
    shares = (kept / total[:, None]).astype(jnp.bfloat16)

    returned = lax.all_to_all(
        shares.reshape(clusters, capacity, quarter),
        "cluster",
        split_axis=0,
        concat_axis=0,
        tiled=True,
    )
    return jnp.dot(
        placed.T, returned.reshape(slots, quarter), preferred_element_type=jnp.float32
    ).astype(returned.dtype)


def solution(mesh):
    in_specs = (
        P("cluster", "feat"),
        P("cluster", None),
        P(),
        P(("cluster", "feat"), None),
        P(("cluster", "feat"), None),
        P(("cluster", "feat")),
    )
    out_specs = P("cluster", "feat")
    return jax.shard_map(body, mesh=mesh, in_specs=in_specs, out_specs=out_specs, check_vma=False)
```

```python
import math

import jax
import jax.numpy as jnp
from jax import lax
from jax.sharding import PartitionSpec as P

REACH = 3


temper = 2.0


def shifted(array, axis, by):
    peers = lax.axis_size(axis)
    return lax.ppermute(array, axis, [(i, (i - by) % peers) for i in range(peers)])


def swapped(array, axis, bit):
    peers = lax.axis_size(axis)
    return lax.ppermute(array, axis, [(i, i ^ bit) for i in range(peers)])


def round_bf16(x):
    return lax.reduce_precision(x, exponent_bits=8, mantissa_bits=7)


def split3(x):
    hi = round_bf16(x)
    rest = x - hi
    mid = round_bf16(rest)
    lo = rest - mid
    return [part.astype(jnp.bfloat16) for part in (hi, mid, lo)]


def join3(parts):
    hi, mid, lo = [p.astype(jnp.float32) for p in parts]
    return (hi + mid) + lo


def merge(kept, top, total, message, width):
    other = message.astype(jnp.float32)
    other_top = join3([other[:, width + i] for i in range(3)])
    other_total = join3([other[:, width + 3 + i] for i in range(3)])
    highest = jnp.maximum(top, other_top)
    mine = jnp.exp(top - highest)
    theirs = jnp.exp(other_top - highest)
    merged = kept * mine[:, None] + other * theirs[:, None]
    return merged, highest, total * mine + other_total * theirs


def body(queries, assign, band_mask, keys, labels, prior):
    clusters = lax.axis_size("cluster")
    cluster_index = lax.axis_index("cluster")
    feat_index = lax.axis_index("feat")
    feats = lax.axis_size("feat")
    local_rows = queries.shape[0]
    depth = keys.shape[1]
    classes = labels.shape[1]
    rows = keys.shape[0]
    capacity = 2 * local_rows // clusters
    slots = clusters * capacity

    quarter = classes // feats
    group = -(-(quarter + 6) // 128) * 128
    lane = lax.broadcasted_iota(jnp.int32, (rows, feats * group), 1)
    padded = jnp.pad(labels.reshape(rows, feats, quarter), ((0, 0), (0, 0), (0, group - quarter)))
    grouped = jnp.where(lane == quarter, prior[:, None], padded.reshape(rows, feats * group))
    block = jnp.stack([keys, grouped])
    offsets = [0]
    for reach in sorted(range(1, REACH + 1), key=lambda r: (r == 2, -r)):
        offsets += [reach, -reach]
    early = {o: shifted(block, "cluster", o) for o in offsets[1:] if abs(o) != 2}

    target = assign[:, 0]
    onehot = (target[:, None] == jnp.arange(clusters, dtype=jnp.int32)[None, :]).astype(jnp.int32)
    before = jnp.cumsum(onehot, axis=0) - onehot
    position = target * capacity + jnp.sum(before * onehot, axis=1)
    placed = (lax.broadcasted_iota(jnp.int32, (slots, local_rows), 0) == position[None, :]).astype(queries.dtype)
    outgoing = jnp.dot(placed, queries, preferred_element_type=jnp.float32).astype(queries.dtype)
    arrived = lax.all_to_all(
        outgoing.reshape(clusters, capacity, queries.shape[1]),
        "cluster",
        split_axis=0,
        concat_axis=0,
        tiled=True,
    )
    own = arrived.reshape(slots, queries.shape[1])
    far = swapped(own, "feat", 2)
    late_block, own = lax.optimization_barrier((block, own))
    early.update({o: shifted(late_block, "cluster", o) for o in offsets[1:] if abs(o) == 2})
    blocks = [block] + [early[o] for o in offsets[1:]]
    near = swapped(jnp.stack([own, far]), "feat", 1)
    width = queries.shape[1]
    query_full = jnp.zeros((slots, feats * width), queries.dtype)
    for part, code in ((own, 0), (far, 2), (near[0], 1), (near[1], 3)):
        query_full = lax.dynamic_update_slice_in_dim(query_full, part, (feat_index ^ code) * width, axis=1)

    band_keys = jnp.stack([b[0] for b in blocks]).reshape(len(offsets) * rows, depth)
    band_labels = jnp.stack([b[1] for b in blocks]).reshape(len(offsets) * rows, feats * group)
    band_prior = band_labels[:, quarter]
    mask_row = band_mask[cluster_index]
    live_blocks = jnp.stack([mask_row[REACH + o] > 0 for o in offsets])
    live = jnp.repeat(live_blocks, rows)
    scale = temper / math.sqrt(depth)
    scores = jnp.einsum("qd,kd->qk", query_full, band_keys, preferred_element_type=jnp.float32) * scale
    scores = scores + band_prior.astype(jnp.float32)[None, :]
    scores = jnp.where(live[None, :], scores, -jnp.inf)
    top = jnp.max(scores, axis=1)
    weight = jnp.exp(scores - top[:, None])
    total = jnp.sum(weight, axis=1)
    accum = jnp.dot(weight.astype(jnp.bfloat16), band_labels, preferred_element_type=jnp.float32)

    column = lax.broadcasted_iota(jnp.int32, (slots, group), 1)

    def pack(part, top, total):
        for i, c in enumerate(split3(top) + split3(total)):
            part = jnp.where(column == quarter + i, c.astype(jnp.float32)[:, None], part)
        return part.astype(jnp.bfloat16)

    grid = accum.reshape(slots, feats, group)
    pick = lambda g: lax.dynamic_index_in_dim(grid, g, axis=1, keepdims=False)
    kept = jnp.stack([pick(feat_index), pick(feat_index ^ 2)])
    sent = jnp.stack([pack(pick(feat_index ^ 1), top, total), pack(pick(feat_index ^ 3), top, total)])
    message = swapped(sent, "feat", 1).astype(jnp.float32)
    other_top = join3([message[0, :, quarter + i] for i in range(3)])
    other_total = join3([message[0, :, quarter + 3 + i] for i in range(3)])
    highest = jnp.maximum(top, other_top)
    mine = jnp.exp(top - highest)
    theirs = jnp.exp(other_top - highest)
    kept = kept * mine[None, :, None] + message * theirs[None, :, None]
    top, total = highest, total * mine + other_total * theirs
    message = swapped(pack(kept[1], top, total), "feat", 2)
    kept, top, total = merge(kept[0], top, total, message, quarter)
    kept = kept[:, :quarter]
    shares = (kept / total[:, None]).astype(jnp.bfloat16)

    returned = lax.all_to_all(
        shares.reshape(clusters, capacity, quarter),
        "cluster",
        split_axis=0,
        concat_axis=0,
        tiled=True,
    )
    return jnp.dot(
        placed.T, returned.reshape(slots, quarter), preferred_element_type=jnp.float32
    ).astype(returned.dtype)


def solution(mesh):
    in_specs = (
        P("cluster", "feat"),
        P("cluster", None),
        P(),
        P(("cluster", "feat"), None),
        P(("cluster", "feat"), None),
        P(("cluster", "feat")),
    )
    out_specs = P("cluster", "feat")
    return jax.shard_map(body, mesh=mesh, in_specs=in_specs, out_specs=out_specs, check_vma=False)
```
